32 devices in a mesh: dp: 1, tensor: 32 (over z, y, x, core).
Axes of the slice: x: 2, y: 2, z: 4, core: 2. Of those that a mesh axis runs over, the one named last changes fastest.
Arguments:
- decode_queries: bfloat16 [1, 32, 2048], P('dp'), may hold values from -17.5 to 17.5
- new_keys: bfloat16 [1, 32, 2048], P('dp'), may hold values from -7 to 7
- new_values: bfloat16 [1, 32, 2048], P('dp'), may hold values from -6 to 6
- cache_keys: bfloat16 [1, 4, 8192, 2048], P('dp', None, 'tensor'), may hold values from -32 to 32
- cache_values: bfloat16 [1, 4, 8192, 2048], P('dp', None, 'tensor'), may hold values from -6 to 6
- group_of: int32 [1, 32], P('dp'), may hold values from 0 to 3, never falling along the last dimension, each value on 1 to 16 neighbouring positions
- cache_lengths: int32 [1, 4], P('dp'), may hold values from 1024 to 8192, as said below
- decode_residual: bfloat16 [1, 32, 2048], P('dp', 'tensor'), may hold values from -3 to 3
- out_weight: bfloat16 [2048, 2048], P('tensor'), may hold values from -0.125 to 0.125
- prefill_states: bfloat16 [2048, 2048], P(('dp', 'tensor')), may hold values from -6 to 6
- norm_gain: float32 [2048], replicated, may hold values from 0.1 to 1.9
- routes: int32 [2080, 8], P(('dp', 'tensor')), may hold values from 0 to 31, all different within a row; in each aligned block of 65 rows (0 to 64, 65 to 129, ...) at most 24 rows name the same one
- route_weights: float32 [2080, 8], P(('dp', 'tensor')), may hold values from 0.05 to 0.5
- w_gate: bfloat16 [32, 2048, 1024], P('tensor', None, 'dp'), may hold values from -0.125 to 0.125
- w_up: bfloat16 [32, 2048, 1024], P('tensor', None, 'dp'), may hold values from -0.125 to 0.125
- w_down: bfloat16 [32, 1024, 2048], P('tensor', 'dp'), may hold values from -0.1875 to 0.1875
Outputs:
- prefill_out: bfloat16 [2048, 2048], P(('dp', 'tensor'))
- decode_out: bfloat16 [1, 32, 2048], P('dp', 'tensor')
The draws below stay inside these ranges and needn't reach their ends.
Inputs may be any that keep to these rules, and one draw needn't show every extreme that they name: `group_of`: groups never fall along the requests of one dp index; each of the 4 groups has 1 to 16 requests, and some group has exactly 16. `cache_lengths`: every group's cache holds an eighth of 8192 positions or more, and in every draw some group holds all 8192. `routes`: the 8 experts of a row differ. Within the rows of one device no expert is named by more than 24 rows, a bound that some block reaches.
All inputs are finite; a program needn't handle non-finite values.
Results may differ from the reference program's by a relative error of at most 0.023.
Values may be sent and summed in bfloat16 or wider, within the bound.
No kernel may reach another device: no remote copies, remote signals or barrier semaphores. Data moves between devices by JAX's collectives and lax.ppermute only.
A program may use at most 128 MiB of HBM per device.

```python
import math
import jax
import jax.numpy as jnp
import numpy as np
from jax import lax

D = 2048
HEADS = 16
HEAD_DIM = 128
FF = 1024
TOPK = 8
TOK_DEV = 64
REQ_DEV = 1
EXPERTS = 32
REQ_DP = 32
GROUPS = 4
CACHE = 8192
ROWS_DEV = 65
CAP = 24
PREFILL = 2048
ROWS = 2080
N_DP = 1
N_TENSOR = 32


def base_queries(key):
    return 3.5 * jax.random.truncated_normal(jax.random.fold_in(key, 11), -5.0, 5.0, (N_DP, REQ_DP, D), jnp.float32)


def draw_decode_queries(key, part):
    return base_queries(key).astype(jnp.bfloat16)


def draw_new_keys(key, part):
    queries = base_queries(key)
    noise = jax.random.truncated_normal(jax.random.fold_in(key, 12), -5.0, 5.0, (N_DP, REQ_DP, D), jnp.float32)
    return (0.09 * queries + noise).astype(jnp.bfloat16)


def draw_cache_keys(key, part):
    shape = (N_DP, GROUPS, CACHE, D)
    table = jax.random.truncated_normal(jax.random.fold_in(key, 13), -5.0, 5.0, shape, jnp.float32)
    return table.astype(jnp.bfloat16)


def draw_cache_lengths(key, part):
    reach = CACHE - CACHE // 8 + 1
    lengths = CACHE // 8 + jax.random.randint(jax.random.fold_in(key, 21), (N_DP * GROUPS,), 0, reach)
    chosen = jax.random.randint(jax.random.fold_in(key, 22), (), 0, N_DP * GROUPS)
    lengths = lengths.at[chosen].set(CACHE)
    return lengths.reshape(N_DP, GROUPS).astype(jnp.int32)


def steps_of(rng, shape, shards, smallest, top_value):
    def one(axis_at, shards_of):
        steps = jax.random.uniform(jax.random.fold_in(jax.random.fold_in(rng, 6), axis_at), (shards_of,), jnp.float32, smallest / len(shards), top_value / len(shards))
        return jnp.repeat(jnp.exp(steps), shape[axis_at] // shards_of).reshape((-1,) + (1,) * (len(shape) - axis_at - 1))

    factor_of = one(*shards[0])
    for cut in shards[1:]:
        factor_of = factor_of * one(*cut)
    return factor_of


def length_profile(amount, total, most, skew):
    weights = [(1 << 20) // math.isqrt(grade ** skew) + 1 for grade in range(2, amount + 1)]
    surplus, given = total - most - (amount - 1), [1] * (amount - 1)
    while surplus > 0:
        free = [i for i in range(amount - 1) if given[i] < most]
        whole, left = sum([weights[i] for i in free]), surplus
        for i in free:
            more = min(most - given[i], max(1, left * weights[i] // whole), surplus)
            given[i] = given[i] + more
            surplus = surplus - more
    return np.array([most] + given)


def ragged_sizes(rng, count, total, bound, lean):
    if count == 2:
        one = jax.random.randint(rng, (), max(1, total - bound), min(bound, total - 1) + 1)
        return jnp.stack([one, total - one])
    tallies = jnp.asarray(length_profile(count, total, bound, lean), jnp.int32)
    pairs = (count - 1) // 2
    donor, receiver = tallies[1:1 + 2 * pairs:2], tallies[2:2 + 2 * pairs:2]
    room = jnp.minimum(donor - 1, bound - receiver)
    shifted = jax.random.randint(jax.random.fold_in(rng, 1), (pairs,), 0, 1 << 20) % (room + 1)
    tallies = tallies.at[1:1 + 2 * pairs:2].set(donor - shifted).at[2:2 + 2 * pairs:2].set(receiver + shifted)
    return tallies[jax.random.permutation(jax.random.fold_in(rng, 2), count)]


def deal_out(key, own, number, rows, amount, top, bound, slope):
    order = jax.random.permutation(key, amount)
    packed, ordinary = shares(amount, rows * top, bound, slope, True), shares(amount, rows * top, bound, slope, False)
    places = jnp.arange(amount)

    def named(sizes, turn):
        used = int((sizes > 0).sum())
        fixed = max(1, used // 4)
        moved = fixed + (places - fixed + turn * (used - fixed)) % max(1, amount - fixed)
        return jnp.zeros((amount,), jnp.int32).at[order[jnp.where(places < fixed, places, moved)]].set(jnp.asarray(sizes, jnp.int32))

    sizes = jnp.where(number % 4 == 0, named(packed, number // 4), named(ordinary, number - number // 4 - 1))
    mixed = jax.random.permutation(jax.random.fold_in(own, 3), amount)
    source_of, receiver = mixed[0:amount // 2 * 2:2], mixed[1:amount // 2 * 2:2]
    room = jnp.minimum(sizes[source_of] - 1, bound - sizes[receiver]) // 2
    room = jnp.where((source_of == order[0]) | (receiver == order[0]) | (sizes[receiver] == 0), 0, jnp.maximum(room, 0))
    moved = jax.random.randint(jax.random.fold_in(own, 4), (amount // 2,), 0, 1 << 20) % (room + 1)
    sizes = sizes.at[source_of].add(-moved).at[receiver].add(moved)
    labels = jnp.searchsorted(jnp.cumsum(sizes), jnp.arange(rows * top), side="right").astype(jnp.int32)
    listing = labels.reshape(top, rows).T
    listing = listing[jax.random.permutation(jax.random.fold_in(own, 1), rows)]
    turn = jax.random.randint(jax.random.fold_in(own, 2), (rows, 1), 0, top)
    return jnp.take_along_axis(listing, (jnp.arange(top)[None, :] + turn) % top, axis=1)


def shares(count, total, bound, skew, full):
    loads = [(1 << 20) // math.isqrt(rank ** skew) + 1 for rank in range(1, count + 1)]
    largest = bound if full else min(bound, max(-(-total // count), total * loads[0] // sum(loads)))
    least = 1 if total - largest >= count - 1 else 0
    holding, surplus = [largest] + [least] * (count - 1), total - largest - least * (count - 1)
    while surplus > 0:
        free = [i for i in range(1, count) if holding[i] < largest] or [i for i in range(1, count) if holding[i] < bound]
        mass, remaining = sum([loads[i] for i in free]), surplus
        for i in free:
            more = min(bound - holding[i], max(1, remaining * loads[i] // mass), surplus)
            holding[i] = holding[i] + more
            surplus = surplus - more
    return np.array(holding)


def bell_draw(key, shape, spread, most, cuts=(), kind=jnp.bfloat16):
    entries = jax.random.normal(key, shape, jnp.float32) * spread
    if len(cuts) > 0:
        entries = steps_of(key, shape, cuts, -0.22, 0.18) * entries
    return jnp.clip(entries, min=-most, max=most).astype(kind)


def setup_inputs(seed: int = 0) -> dict:
    key_of = jax.random.split(jax.random.key(seed), 17)
    decode_queries = draw_decode_queries(jax.random.fold_in(key_of[16], 71), 0)
    new_keys = draw_new_keys(jax.random.fold_in(key_of[16], 71), 0)
    new_values = bell_draw(key_of[2], (N_DP, REQ_DP, D), 1.0, 6.0)
    cache_keys = draw_cache_keys(jax.random.fold_in(key_of[16], 71), 0)
    cache_values = bell_draw(key_of[4], (N_DP, GROUPS, CACHE, D), 1.0, 6.0, ((2, 32),))
    group_of = jax.vmap(lambda own: jnp.searchsorted(jnp.cumsum(ragged_sizes(own, GROUPS, REQ_DP, 16, 1)), jnp.arange(REQ_DP), side="right"))(jax.random.split(key_of[5], N_DP)).reshape((N_DP, REQ_DP)).astype(jnp.int32)
    cache_lengths = draw_cache_lengths(jax.random.fold_in(key_of[16], 71), 0)
    decode_residual = bell_draw(key_of[7], (N_DP, REQ_DP, D), 0.5, 3.0, ((1, 32),))
    out_weight = bell_draw(key_of[8], (D, D), D ** -0.5, 0.125, ((0, 32),))
    prefill_states = bell_draw(key_of[9], (PREFILL, D), 1.0, 6.0, ((0, 32),))
    norm_gain = jnp.clip(1.0 + 0.18 * jax.random.normal(key_of[10], (D,), jnp.float32), 0.1, 1.9)
    routes_keys = jax.random.split(jax.random.fold_in(key_of[11], 1), ROWS // ROWS_DEV)
    routes_turns = jax.random.permutation(jax.random.fold_in(key_of[11], 3), ROWS // ROWS_DEV)
    routes = jax.vmap(lambda own, number: deal_out(jax.random.fold_in(key_of[11], 2), own, number, ROWS_DEV, EXPERTS, TOPK, CAP, 2))(routes_keys, routes_turns).reshape((ROWS, TOPK))
    route_weights = jnp.clip(jnp.exp(math.log(0.5) - 2.3025851 * jax.random.uniform(key_of[12], (ROWS, TOPK), jnp.float32) ** steps_of(key_of[12], (ROWS, TOPK), ((0, 32),), -0.2, 0.2)), 0.05, 0.5)
    w_gate = bell_draw(key_of[13], (EXPERTS, D, FF), D ** -0.5, 0.125, ((0, 32),))
    w_up = bell_draw(key_of[14], (EXPERTS, D, FF), D ** -0.5, 0.125, ((0, 32),))
    w_down = bell_draw(key_of[15], (EXPERTS, FF, D), FF ** -0.5, 0.1875, ((0, 32),))
    return {"decode_queries": decode_queries, "new_keys": new_keys, "new_values": new_values, "cache_keys": cache_keys, "cache_values": cache_values, "group_of": group_of, "cache_lengths": cache_lengths, "decode_residual": decode_residual, "out_weight": out_weight, "prefill_states": prefill_states, "norm_gain": norm_gain, "routes": routes, "route_weights": route_weights, "w_gate": w_gate, "w_up": w_up, "w_down": w_down}


def attend_request(flat_index, decode_queries, new_keys, new_values, cache_keys, cache_values, group_of, cache_lengths):
    batch_index = flat_index // REQ_DP
    request = flat_index % REQ_DP
    group = group_of[batch_index, request]
    key_rows = cache_keys[batch_index, group].astype(jnp.float32).reshape(CACHE, HEADS, HEAD_DIM)
    value_rows = cache_values[batch_index, group].astype(jnp.float32).reshape(CACHE, HEADS, HEAD_DIM)
    query = decode_queries[batch_index, request].astype(jnp.float32).reshape(HEADS, HEAD_DIM)
    own_key = new_keys[batch_index, request].astype(jnp.float32).reshape(HEADS, HEAD_DIM)
    own_value = new_values[batch_index, request].astype(jnp.float32).reshape(HEADS, HEAD_DIM)
    factor = 1.0 / math.sqrt(HEAD_DIM)
    scores = jnp.einsum('hd,jhd->hj', query, key_rows) * factor
    own_score = lax.optimization_barrier(jnp.sum(query * own_key, axis=1)) * factor
    visible = (jnp.arange(CACHE, dtype=jnp.int32) < cache_lengths[batch_index, group])[None, :]
    peak = jnp.maximum(lax.optimization_barrier(jnp.max(jnp.where(visible, scores, -jnp.inf), axis=1)), own_score)
    expon = jnp.where(visible, jnp.exp(scores - peak[:, None]), 0.0)
    own_exp = jnp.exp(own_score - peak)
    totals = lax.optimization_barrier(jnp.sum(expon, axis=1)) + own_exp
    probs = lax.optimization_barrier(expon.astype(jnp.bfloat16)).astype(jnp.float32)
    own_prob = lax.optimization_barrier(own_exp.astype(jnp.bfloat16)).astype(jnp.float32)
    mixture = jnp.einsum('hj,jhd->hd', probs, value_rows) + own_prob[:, None] * own_value
    return (mixture / totals[:, None]).reshape(D).astype(jnp.bfloat16)

def reference(decode_queries, new_keys, new_values, cache_keys, cache_values, group_of, cache_lengths, decode_residual, out_weight, prefill_states, norm_gain, routes, route_weights, w_gate, w_up, w_down):

    def attend_one(flat_index):
        return attend_request(flat_index, decode_queries, new_keys, new_values, cache_keys, cache_values, group_of, cache_lengths)
    attended = lax.map(attend_one, jnp.arange(N_DP * REQ_DP, dtype=jnp.int32))
    projected = jnp.dot(attended, out_weight, preferred_element_type=jnp.float32)
    decode_hidden = (decode_residual.reshape(N_DP * REQ_DP, D).astype(jnp.float32) + projected).astype(jnp.bfloat16)
    prefill_blocks = prefill_states.reshape(N_DP * N_TENSOR, TOK_DEV, D)
    decode_blocks = decode_hidden.reshape(N_DP * N_TENSOR, REQ_DEV, D)
    residual_rows = jnp.concatenate([prefill_blocks, decode_blocks], axis=1).reshape(ROWS, D)
    row_float = residual_rows.astype(jnp.float32)
    inverse = lax.rsqrt(lax.optimization_barrier(jnp.mean(row_float * row_float, axis=1, keepdims=True)) + 1e-06)
    normed = (row_float * inverse * norm_gain).astype(jnp.bfloat16)
    flat_expert = routes.reshape(-1).astype(jnp.int32)
    flat_weight = route_weights.reshape(-1)
    order = jnp.argsort(flat_expert, stable=True).astype(jnp.int32)
    counts = lax.optimization_barrier(jnp.sum((flat_expert[:, None] == jnp.arange(EXPERTS, dtype=jnp.int32)[None, :]).astype(jnp.int32), axis=0)).astype(jnp.int32)
    starts = (jnp.cumsum(counts) - counts).astype(jnp.int32)
    most_rows = N_DP * N_TENSOR * CAP
    order_padded = jnp.concatenate([order, jnp.zeros((most_rows,), jnp.int32)])

    def expert_step(accum, expert):
        picked = lax.dynamic_slice(order_padded, (starts[expert],), (most_rows,))
        valid = jnp.arange(most_rows, dtype=jnp.int32) < counts[expert]
        row_index = (picked // TOPK).astype(jnp.int32)
        inputs = normed[row_index]
        gate = jnp.dot(inputs, w_gate[expert], preferred_element_type=jnp.float32)
        upper = jnp.dot(inputs, w_up[expert], preferred_element_type=jnp.float32)
        active = (jax.nn.silu(gate) * upper).astype(jnp.bfloat16)
        result = jnp.dot(active, w_down[expert], preferred_element_type=jnp.float32).astype(jnp.bfloat16)
        result = lax.optimization_barrier(result).astype(jnp.float32)
        scaled = jnp.where(valid, flat_weight[picked], 0.0)
        accum = accum.at[row_index].add(scaled[:, None] * result)
        return (accum, None)
    accum, unused = lax.scan(expert_step, jnp.zeros((ROWS, D), jnp.float32), jnp.arange(EXPERTS, dtype=jnp.int32))
    mixed_rows = (row_float + accum).astype(jnp.bfloat16).reshape(N_DP * N_TENSOR, ROWS_DEV, D)
    prefill_out = mixed_rows[:, :TOK_DEV].reshape(PREFILL, D)
    decode_out = mixed_rows[:, TOK_DEV:].reshape(N_DP, REQ_DP, D)
    return (prefill_out, decode_out)
```

```python
import math

import jax
import jax.numpy as jnp
from jax import lax
from jax.sharding import PartitionSpec as P

HEADS = 16
HEAD_DIM = 128


def expert_mlp(inputs, gate_w, up_w, down_w):
    flat_rows = inputs.reshape(-1, inputs.shape[-1])
    gate = jnp.dot(flat_rows, gate_w, preferred_element_type=jnp.float32)
    upper = jnp.dot(flat_rows, up_w, preferred_element_type=jnp.float32)
    active = (jax.nn.silu(gate) * upper).astype(jnp.bfloat16)
    return jnp.dot(active, down_w, preferred_element_type=jnp.float32)


def attention_rows(
    decode_queries,
    new_keys,
    new_values,
    cache_keys,
    cache_values,
    group_of,
    cache_lengths,
    decode_residual,
    out_weight,
):
    tensor_count = lax.axis_size("tensor")
    tensor_rank = lax.axis_index("tensor")
    requests = decode_queries.shape[1]
    groups = cache_keys.shape[1]
    reach = cache_keys.shape[2]
    model_width = decode_queries.shape[2]
    width = out_weight.shape[0]
    assert HEAD_DIM % width == 0
    factor = 1.0 / math.sqrt(HEAD_DIM)
    query_heads = decode_queries[0].reshape(requests, HEADS, HEAD_DIM)
    key_table = cache_keys[0].reshape(groups, reach, HEADS, HEAD_DIM)
    value_table = cache_values[0].reshape(groups, reach, HEADS, HEAD_DIM)
    scores = (
        jnp.einsum("rhd,gjhd->grhj", query_heads, key_table, preferred_element_type=jnp.float32)
        * factor
    )
    positions = tensor_rank * reach + jnp.arange(reach, dtype=jnp.int32)
    member = group_of[0][None, :] == jnp.arange(groups, dtype=jnp.int32)[:, None]
    within = positions[None, :] < cache_lengths[0][:, None]
    visible = (member[:, :, None] & within[:, None, :])[:, :, None, :]
    own_keys = new_keys[0].astype(jnp.float32).reshape(requests, HEADS, HEAD_DIM)
    own_score = jnp.sum(query_heads.astype(jnp.float32) * own_keys, axis=2) * factor
    local_peak = jnp.maximum(jnp.max(jnp.where(visible, scores, -jnp.inf), axis=(0, 3)), own_score)
    expon = jnp.where(visible, jnp.exp(scores - local_peak[None, :, :, None]), 0.0)
    probs = expon.astype(jnp.bfloat16)
    local_totals = jnp.sum(expon, axis=(0, 3))
    mixture = jnp.einsum(
        "grhj,gjhd->rhd", probs, value_table, preferred_element_type=jnp.float32
    ).reshape(requests, tensor_count, width)
    head_of = (jnp.arange(tensor_count, dtype=jnp.int32) * width) // HEAD_DIM
    peak_to = local_peak.T[head_of]
    totals_to = local_totals.T[head_of]
    payload = jnp.concatenate(
        [jnp.transpose(mixture, (1, 0, 2)), peak_to[:, :, None], totals_to[:, :, None]], axis=2
    )
    received = lax.all_to_all(payload, "tensor", 0, 0, tiled=True)
    part_mix = received[:, :, :width]
    part_peak = received[:, :, width]
    part_totals = received[:, :, width + 1]
    peak = jnp.max(part_peak, axis=0)
    scale = jnp.exp(part_peak - peak[None, :])
    my_head = (tensor_rank * width) // HEAD_DIM
    first_column = tensor_rank * width
    own_here = lax.dynamic_index_in_dim(own_score, my_head, axis=1, keepdims=False)
    own_exp = jnp.exp(own_here - peak)
    own_prob = lax.optimization_barrier(own_exp.astype(jnp.bfloat16)).astype(jnp.float32)
    totals = jnp.sum(scale * part_totals, axis=0) + own_exp
    own_values = lax.dynamic_slice_in_dim(new_values[0], first_column, width, 1).astype(jnp.float32)
    summed_mix = jnp.sum(scale[:, :, None] * part_mix, axis=0) + own_prob[:, None] * own_values
    attended = (summed_mix / totals[:, None]).astype(jnp.bfloat16)
    partial = jnp.dot(attended, out_weight, preferred_element_type=jnp.float32)
    per_device = requests // tensor_count
    gathered = lax.all_to_all(
        partial.reshape(tensor_count, per_device, model_width), "tensor", 0, 0, tiled=True
    )
    projected = jnp.sum(gathered, axis=0)
    return (decode_residual[0].astype(jnp.float32) + projected).astype(jnp.bfloat16)


def per_device(
    decode_queries,
    new_keys,
    new_values,
    cache_keys,
    cache_values,
    group_of,
    cache_lengths,
    decode_residual,
    out_weight,
    prefill_states,
    norm_gain,
    routes,
    route_weights,
    w_gate,
    w_up,
    w_down,
):
    tensor_count = lax.axis_size("tensor")
    model_width = decode_queries.shape[2]
    decode_hidden = attention_rows(
        decode_queries,
        new_keys,
        new_values,
        cache_keys,
        cache_values,
        group_of,
        cache_lengths,
        decode_residual,
        out_weight,
    )
    residual_rows = jnp.concatenate([prefill_states, decode_hidden], axis=0)
    row_float = residual_rows.astype(jnp.float32)
    inverse = lax.rsqrt(jnp.mean(row_float * row_float, axis=1, keepdims=True) + 1e-06)
    normed = (row_float * inverse * norm_gain).astype(jnp.bfloat16)
    row_count, top_count = routes.shape
    capacity = max(8, (row_count * top_count * 3 // (2 * tensor_count) + 7) // 8 * 8)
    flat_expert = routes.reshape(-1)
    one_hot = (flat_expert[:, None] == jnp.arange(tensor_count, dtype=jnp.int32)[None, :]).astype(
        jnp.int32
    )
    earlier = jnp.cumsum(one_hot, axis=0) - one_hot
    rank_within = jnp.sum(earlier * one_hot, axis=1)
    slot_index = flat_expert * capacity + rank_within
    slots = jnp.arange(tensor_count * capacity, dtype=jnp.int32)
    select = jnp.any(
        slot_index.reshape(row_count, top_count)[None, :, :] == slots[:, None, None], axis=2
    ).astype(jnp.bfloat16)
    outgoing = jnp.dot(select, normed, preferred_element_type=jnp.float32).astype(jnp.bfloat16)
    outgoing = outgoing.reshape(tensor_count, capacity, model_width)
    both_groups = lax.all_gather(
        lax.all_to_all(outgoing, "tensor", split_axis=0, concat_axis=0, tiled=True),
        "dp",
        axis=0,
        tiled=True,
    )
    block = both_groups
    returned = lax.all_to_all(
        lax.psum_scatter(
            expert_mlp(block, w_gate[0], w_up[0], w_down[0])
            .reshape(block.shape)
            .astype(jnp.bfloat16),
            "dp",
            scatter_dimension=0,
            tiled=True,
        ),
        "tensor",
        split_axis=0,
        concat_axis=0,
        tiled=True,
    )
    gathered = returned.reshape(tensor_count * capacity, model_width)[slot_index].astype(
        jnp.float32
    )
    weighted = jnp.sum(
        (gathered * route_weights.reshape(-1)[:, None]).reshape(row_count, top_count, model_width),
        axis=1,
    )
    mixed_rows = (row_float + weighted).astype(jnp.bfloat16)
    prefill_count = prefill_states.shape[0]
    return (mixed_rows[:prefill_count], mixed_rows[prefill_count:][None])


def solution(mesh):
    in_specs = (
        P("dp", None, None),
        P("dp", None, None),
        P("dp", None, None),
        P("dp", None, "tensor", None),
        P("dp", None, "tensor", None),
        P("dp", None),
        P("dp", None),
        P("dp", "tensor", None),
        P("tensor", None),
        P(("dp", "tensor"), None),
        P(),
        P(("dp", "tensor"), None),
        P(("dp", "tensor"), None),
        P("tensor", None, "dp"),
        P("tensor", None, "dp"),
        P("tensor", "dp", None),
    )
    out_specs = (P(("dp", "tensor"), None), P("dp", "tensor", None))
    return jax.shard_map(
        per_device, mesh=mesh, in_specs=in_specs, out_specs=out_specs, check_vma=False
    )
```

```python
import math

import jax
import jax.numpy as jnp
from jax import lax
from jax.sharding import PartitionSpec as P

HEADS = 16
HEAD_DIM = 128


def expert_mlp(inputs, gate_w, up_w, down_w):
    flat_rows = inputs.reshape(-1, inputs.shape[-1])
    gate = jnp.dot(flat_rows, gate_w, preferred_element_type=jnp.float32)
    upper = jnp.dot(flat_rows, up_w, preferred_element_type=jnp.float32)
    active = (jax.nn.silu(gate) * upper).astype(jnp.bfloat16)
    return jnp.dot(active, down_w, preferred_element_type=jnp.float32)


def attention_partials(
    decode_queries, new_keys, cache_keys, cache_values, group_of, cache_lengths, width
):
    tensor_count = lax.axis_size("tensor")
    tensor_rank = lax.axis_index("tensor")
    requests = decode_queries.shape[1]
    groups = cache_keys.shape[1]
    reach = cache_keys.shape[2]
    assert HEAD_DIM % width == 0
    factor = 1.0 / math.sqrt(HEAD_DIM)
    query_heads = decode_queries[0].reshape(requests, HEADS, HEAD_DIM)
    key_table = cache_keys[0].reshape(groups, reach, HEADS, HEAD_DIM)
    value_table = cache_values[0].reshape(groups, reach, HEADS, HEAD_DIM)
    scores = (
        jnp.einsum("rhd,gjhd->grhj", query_heads, key_table, preferred_element_type=jnp.float32)
        * factor
    )
    positions = tensor_rank * reach + jnp.arange(reach, dtype=jnp.int32)
    member = group_of[0][None, :] == jnp.arange(groups, dtype=jnp.int32)[:, None]
    within = positions[None, :] < cache_lengths[0][:, None]
    visible = (member[:, :, None] & within[:, None, :])[:, :, None, :]
    own_keys = new_keys[0].astype(jnp.float32).reshape(requests, HEADS, HEAD_DIM)
    own_score = jnp.sum(query_heads.astype(jnp.float32) * own_keys, axis=2) * factor
    local_peak = jnp.maximum(jnp.max(jnp.where(visible, scores, -jnp.inf), axis=(0, 3)), own_score)
    expon = jnp.where(visible, jnp.exp(scores - local_peak[None, :, :, None]), 0.0)
    probs = expon.astype(jnp.bfloat16)
    local_totals = jnp.sum(expon, axis=(0, 3))
    mixture = jnp.einsum(
        "grhj,gjhd->rhd", probs, value_table, preferred_element_type=jnp.float32
    ).reshape(requests, tensor_count, width)
    head_of = (jnp.arange(tensor_count, dtype=jnp.int32) * width) // HEAD_DIM
    peak_to = local_peak.T[head_of]
    totals_to = local_totals.T[head_of]
    payload = jnp.concatenate(
        [jnp.transpose(mixture, (1, 0, 2)), peak_to[:, :, None], totals_to[:, :, None]], axis=2
    )
    return payload, own_score


def attention_finish(received, own_score, new_values, decode_residual, out_weight):
    tensor_count = lax.axis_size("tensor")
    tensor_rank = lax.axis_index("tensor")
    requests, model_width = new_values.shape[1], new_values.shape[2]
    width = out_weight.shape[0]
    part_mix = received[:, :, :width]
    part_peak = received[:, :, width]
    part_totals = received[:, :, width + 1]
    peak = jnp.max(part_peak, axis=0)
    scale = jnp.exp(part_peak - peak[None, :])
    my_head = (tensor_rank * width) // HEAD_DIM
    first_column = tensor_rank * width
    own_here = lax.dynamic_index_in_dim(own_score, my_head, axis=1, keepdims=False)
    own_exp = jnp.exp(own_here - peak)
    own_prob = lax.optimization_barrier(own_exp.astype(jnp.bfloat16)).astype(jnp.float32)
    totals = jnp.sum(scale * part_totals, axis=0) + own_exp
    own_values = lax.dynamic_slice_in_dim(new_values[0], first_column, width, 1).astype(jnp.float32)
    summed_mix = jnp.sum(scale[:, :, None] * part_mix, axis=0) + own_prob[:, None] * own_values
    attended = (summed_mix / totals[:, None]).astype(jnp.bfloat16)
    partial = jnp.dot(attended, out_weight, preferred_element_type=jnp.float32)
    per_device = requests // tensor_count
    gathered = lax.all_to_all(
        partial.reshape(tensor_count, per_device, model_width), "tensor", 0, 0, tiled=True
    )
    projected = jnp.sum(gathered, axis=0)
    return (decode_residual[0].astype(jnp.float32) + projected).astype(jnp.bfloat16)


def rms_normed(residual_rows, norm_gain):
    row_float = residual_rows.astype(jnp.float32)
    inverse = lax.rsqrt(jnp.mean(row_float * row_float, axis=1, keepdims=True) + 1e-06)
    return row_float, (row_float * inverse * norm_gain).astype(jnp.bfloat16)


def dispatch(normed, slot_index, slot_count):
    row_count = normed.shape[0]
    slots = jnp.arange(slot_count, dtype=jnp.int32)
    select = jnp.any(
        slot_index.reshape(row_count, -1)[None, :, :] == slots[:, None, None], axis=2
    ).astype(jnp.bfloat16)
    outgoing = jnp.dot(select, normed, preferred_element_type=jnp.float32).astype(jnp.bfloat16)
    tensor_count = lax.axis_size("tensor")
    outgoing = outgoing.reshape(tensor_count, slot_count // tensor_count, normed.shape[1])
    return lax.all_to_all(outgoing, "tensor", split_axis=0, concat_axis=0, tiled=True)


def experts_on(received, experts):
    block = lax.all_gather(received, "dp", axis=0, tiled=True)
    return expert_mlp(block, *experts).reshape(block.shape).astype(jnp.bfloat16)


def rank_in_expert(flat_expert, tensor_count):
    one_hot = (flat_expert[:, None] == jnp.arange(tensor_count, dtype=jnp.int32)[None, :]).astype(
        jnp.int32
    )
    earlier = jnp.cumsum(one_hot, axis=0) - one_hot
    return jnp.sum(earlier * one_hot, axis=1)


def per_device(
    decode_queries,
    new_keys,
    new_values,
    cache_keys,
    cache_values,
    group_of,
    cache_lengths,
    decode_residual,
    out_weight,
    prefill_states,
    norm_gain,
    routes,
    route_weights,
    w_gate,
    w_up,
    w_down,
):
    tensor_count = lax.axis_size("tensor")
    model_width = decode_queries.shape[2]
    prefill_count = prefill_states.shape[0]
    row_count, top_count = routes.shape
    decode_count = row_count - prefill_count
    capacity = max(8, (row_count * top_count * 3 // (2 * tensor_count) + 7) // 8 * 8)
    stride = capacity + decode_count
    experts = (w_gate[0], w_up[0], w_down[0])
    prefill_routes = routes[:prefill_count].reshape(-1)
    decode_routes = routes[prefill_count:]
    prefill_rank = rank_in_expert(prefill_routes, tensor_count)
    prefill_float, prefill_normed = rms_normed(prefill_states, norm_gain)
    prefill_in = dispatch(
        prefill_normed, prefill_routes * capacity + prefill_rank, tensor_count * capacity
    )
    payload, own_score = attention_partials(
        decode_queries, new_keys, cache_keys, cache_values, group_of, cache_lengths,
        out_weight.shape[0],
    )
    payload, prefill_in = lax.optimization_barrier((payload, prefill_in))
    received = lax.all_to_all(payload, "tensor", 0, 0, tiled=True)
    prefill_done = experts_on(prefill_in, experts)
    decode_hidden = attention_finish(received, own_score, new_values, decode_residual, out_weight)
    decode_float, decode_normed = rms_normed(decode_hidden, norm_gain)
    decode_slot = decode_routes * decode_count + jnp.arange(decode_count, dtype=jnp.int32)[:, None]
    decode_in = dispatch(decode_normed, decode_slot.reshape(-1), tensor_count * decode_count)
    decode_done = experts_on(decode_in, experts)
    merged = jnp.concatenate([prefill_done, decode_done], axis=1)
    returned = lax.all_to_all(
        lax.psum_scatter(merged, "dp", scatter_dimension=0, tiled=True),
        "tensor",
        split_axis=0,
        concat_axis=0,
        tiled=True,
    ).reshape(tensor_count * stride, model_width)
    place = jnp.concatenate(
        [
            prefill_routes.reshape(prefill_count, top_count) * stride
            + prefill_rank.reshape(prefill_count, top_count),
            decode_routes * stride + capacity
            + jnp.arange(decode_count, dtype=jnp.int32)[:, None],
        ],
        axis=0,
    )
    columns = jnp.arange(tensor_count * stride, dtype=jnp.int32)
    mixing = jnp.sum(
        jnp.where(place[:, :, None] == columns[None, None, :], route_weights[:, :, None], 0.0),
        axis=1,
    )
    high = mixing.astype(jnp.bfloat16)
    rest = mixing - high.astype(jnp.float32)
    middle = rest.astype(jnp.bfloat16)
    low = (rest - middle.astype(jnp.float32)).astype(jnp.bfloat16)
    parts = jnp.dot(
        jnp.concatenate([high, middle, low], axis=0), returned, preferred_element_type=jnp.float32
    ).reshape(3, row_count, model_width)
    weighted = (parts[0] + parts[1]) + parts[2]
    row_float = jnp.concatenate([prefill_float, decode_float], axis=0)
    mixed_rows = (row_float + weighted).astype(jnp.bfloat16)
    return (mixed_rows[:prefill_count], mixed_rows[prefill_count:][None])


def solution(mesh):
    in_specs = (
        P("dp", None, None),
        P("dp", None, None),
        P("dp", None, None),
        P("dp", None, "tensor", None),
        P("dp", None, "tensor", None),
        P("dp", None),
        P("dp", None),
        P("dp", "tensor", None),
        P("tensor", None),
        P(("dp", "tensor"), None),
        P(),
        P(("dp", "tensor"), None),
        P(("dp", "tensor"), None),
        P("tensor", None, "dp"),
        P("tensor", None, "dp"),
        P("tensor", "dp", None),
    )
    out_specs = (P(("dp", "tensor"), None), P("dp", "tensor", None))
    return jax.shard_map(
        per_device, mesh=mesh, in_specs=in_specs, out_specs=out_specs, check_vma=False
    )
```

```python
import math

import jax
import jax.numpy as jnp
from jax import lax
from jax.sharding import PartitionSpec as P

HEADS = 16
HEAD_DIM = 128


def expert_mlp(inputs, gate_w, up_w, down_w):
    flat_rows = inputs.reshape(-1, inputs.shape[-1])
    gate = jnp.dot(flat_rows, gate_w, preferred_element_type=jnp.float32)
    upper = jnp.dot(flat_rows, up_w, preferred_element_type=jnp.float32)
    active = (jax.nn.silu(gate) * upper).astype(jnp.bfloat16)
    return jnp.dot(active, down_w, preferred_element_type=jnp.float32)


def attention_rows(
    decode_queries,
    new_keys,
    new_values,
    cache_keys,
    cache_values,
    group_of,
    cache_lengths,
    decode_residual,
    out_weight,
):
    tensor_count = lax.axis_size("tensor")
    tensor_rank = lax.axis_index("tensor")
    requests = decode_queries.shape[1]
    groups = cache_keys.shape[1]
    reach = cache_keys.shape[2]
    model_width = decode_queries.shape[2]
    width = out_weight.shape[0]
    assert HEAD_DIM % width == 0
    factor = 1.0 / math.sqrt(HEAD_DIM)
    query_heads = decode_queries[0].reshape(requests, HEADS, HEAD_DIM)
    key_table = cache_keys[0].reshape(groups, reach, HEADS, HEAD_DIM)
    value_table = cache_values[0].reshape(groups, reach, HEADS, HEAD_DIM)
    scores = (
        jnp.einsum("rhd,gjhd->grhj", query_heads, key_table, preferred_element_type=jnp.float32)
        * factor
    )
    positions = tensor_rank * reach + jnp.arange(reach, dtype=jnp.int32)
    member = group_of[0][None, :] == jnp.arange(groups, dtype=jnp.int32)[:, None]
    within = positions[None, :] < cache_lengths[0][:, None]
    visible = (member[:, :, None] & within[:, None, :])[:, :, None, :]
    own_keys = new_keys[0].astype(jnp.float32).reshape(requests, HEADS, HEAD_DIM)
    own_score = jnp.sum(query_heads.astype(jnp.float32) * own_keys, axis=2) * factor
    local_peak = jnp.maximum(jnp.max(jnp.where(visible, scores, -jnp.inf), axis=(0, 3)), own_score)
    expon = jnp.where(visible, jnp.exp(scores - local_peak[None, :, :, None]), 0.0)
    probs = expon.astype(jnp.bfloat16)
    local_totals = jnp.sum(expon, axis=(0, 3))
    mixture = jnp.einsum(
        "grhj,gjhd->rhd", probs, value_table, preferred_element_type=jnp.float32
    ).reshape(requests, tensor_count, width)
    head_of = (jnp.arange(tensor_count, dtype=jnp.int32) * width) // HEAD_DIM
    peak_to = local_peak.T[head_of]
    totals_to = local_totals.T[head_of]
    flat_mix = jnp.transpose(mixture, (1, 0, 2)).reshape(tensor_count, requests * width)
    payload = jnp.concatenate([flat_mix, peak_to, totals_to], axis=1)
    received = lax.all_to_all(payload, "tensor", 0, 0, tiled=True)
    mixed_width = requests * width
    part_mix = received[:, :mixed_width].reshape(tensor_count, requests, width)
    part_peak = received[:, mixed_width:mixed_width + requests]
    part_totals = received[:, mixed_width + requests:]
    peak = jnp.max(part_peak, axis=0)
    scale = jnp.exp(part_peak - peak[None, :])
    my_head = (tensor_rank * width) // HEAD_DIM
    first_column = tensor_rank * width
    own_here = lax.dynamic_index_in_dim(own_score, my_head, axis=1, keepdims=False)
    own_exp = jnp.exp(own_here - peak)
    own_prob = lax.optimization_barrier(own_exp.astype(jnp.bfloat16)).astype(jnp.float32)
    totals = jnp.sum(scale * part_totals, axis=0) + own_exp
    own_values = lax.dynamic_slice_in_dim(new_values[0], first_column, width, 1).astype(jnp.float32)
    summed_mix = jnp.sum(scale[:, :, None] * part_mix, axis=0) + own_prob[:, None] * own_values
    attended = (summed_mix / totals[:, None]).astype(jnp.bfloat16)
    partial = jnp.dot(attended, out_weight, preferred_element_type=jnp.float32)
    per_device = requests // tensor_count
    gathered = lax.all_to_all(
        partial.reshape(tensor_count, per_device, model_width), "tensor", 0, 0, tiled=True
    )
    projected = jnp.sum(gathered, axis=0)
    return (decode_residual[0].astype(jnp.float32) + projected).astype(jnp.bfloat16)


def per_device(
    decode_queries,
    new_keys,
    new_values,
    cache_keys,
    cache_values,
    group_of,
    cache_lengths,
    decode_residual,
    out_weight,
    prefill_states,
    norm_gain,
    routes,
    route_weights,
    w_gate,
    w_up,
    w_down,
):
    tensor_count = lax.axis_size("tensor")
    model_width = decode_queries.shape[2]
    decode_hidden = attention_rows(
        decode_queries,
        new_keys,
        new_values,
        cache_keys,
        cache_values,
        group_of,
        cache_lengths,
        decode_residual,
        out_weight,
    )
    residual_rows = jnp.concatenate([prefill_states, decode_hidden], axis=0)
    row_float = residual_rows.astype(jnp.float32)
    inverse = lax.rsqrt(jnp.mean(row_float * row_float, axis=1, keepdims=True) + 1e-06)
    normed = (row_float * inverse * norm_gain).astype(jnp.bfloat16)
    row_count, top_count = routes.shape
    capacity = max(8, (row_count * top_count * 3 // (2 * tensor_count) + 7) // 8 * 8)
    flat_expert = routes.reshape(-1)
    one_hot = (flat_expert[:, None] == jnp.arange(tensor_count, dtype=jnp.int32)[None, :]).astype(
        jnp.int32
    )
    earlier = jnp.cumsum(one_hot, axis=0) - one_hot
    rank_within = jnp.sum(earlier * one_hot, axis=1)
    slot_index = flat_expert * capacity + rank_within
    slots = jnp.arange(tensor_count * capacity, dtype=jnp.int32)
    select = jnp.any(
        slot_index.reshape(row_count, top_count)[None, :, :] == slots[:, None, None], axis=2
    ).astype(jnp.bfloat16)
    outgoing = jnp.dot(select, normed, preferred_element_type=jnp.float32).astype(jnp.bfloat16)
    outgoing = outgoing.reshape(tensor_count, capacity, model_width)
    both_groups = lax.all_gather(
        lax.all_to_all(outgoing, "tensor", split_axis=0, concat_axis=0, tiled=True),
        "dp",
        axis=0,
        tiled=True,
    )
    block = both_groups
    returned = lax.all_to_all(
        lax.psum_scatter(
            expert_mlp(block, w_gate[0], w_up[0], w_down[0])
            .reshape(block.shape)
            .astype(jnp.bfloat16),
            "dp",
            scatter_dimension=0,
            tiled=True,
        ),
        "tensor",
        split_axis=0,
        concat_axis=0,
        tiled=True,
    )
    returned = returned.reshape(tensor_count * capacity, model_width)
    columns = jnp.arange(tensor_count * capacity, dtype=jnp.int32)
    mixing = jnp.sum(
        jnp.where(
            slot_index.reshape(row_count, top_count)[:, :, None] == columns[None, None, :],
            route_weights[:, :, None],
            0.0,
        ),
        axis=1,
    )
    high = mixing.astype(jnp.bfloat16)
    rest = mixing - high.astype(jnp.float32)
    middle = rest.astype(jnp.bfloat16)
    low = (rest - middle.astype(jnp.float32)).astype(jnp.bfloat16)
    prefill_count = prefill_states.shape[0]

    def combined(lo, hi):
        parts = jnp.dot(
            jnp.concatenate([high[lo:hi], middle[lo:hi], low[lo:hi]], axis=0),
            returned,
            preferred_element_type=jnp.float32,
        ).reshape(3, hi - lo, model_width)
        weighted = (parts[0] + parts[1]) + parts[2]
        return (row_float[lo:hi] + weighted).astype(jnp.bfloat16)

    return (combined(0, prefill_count), combined(prefill_count, row_count)[None])


def solution(mesh):
    in_specs = (
        P("dp", None, None),
        P("dp", None, None),
        P("dp", None, None),
        P("dp", None, "tensor", None),
        P("dp", None, "tensor", None),
        P("dp", None),
        P("dp", None),
        P("dp", "tensor", None),
        P("tensor", None),
        P(("dp", "tensor"), None),
        P(),
        P(("dp", "tensor"), None),
        P(("dp", "tensor"), None),
        P("tensor", None, "dp"),
        P("tensor", None, "dp"),
        P("tensor", "dp", None),
    )
    out_specs = (P(("dp", "tensor"), None), P("dp", "tensor", None))
    return jax.shard_map(
        per_device, mesh=mesh, in_specs=in_specs, out_specs=out_specs, check_vma=False
    )
```

```python
import math

import jax
import jax.numpy as jnp
from jax import lax
from jax.sharding import PartitionSpec as P

HEADS = 16
HEAD_DIM = 128


def expert_mlp(inputs, gate_w, up_w, down_w):
    flat_rows = inputs.reshape(-1, inputs.shape[-1])
    gate = jnp.dot(flat_rows, gate_w, preferred_element_type=jnp.float32)
    upper = jnp.dot(flat_rows, up_w, preferred_element_type=jnp.float32)
    active = (jax.nn.silu(gate) * upper).astype(jnp.bfloat16)
    return jnp.dot(active, down_w, preferred_element_type=jnp.float32)


def attention_rows(
    decode_queries,
    new_keys,
    new_values,
    cache_keys,
    cache_values,
    group_of,
    cache_lengths,
    decode_residual,
    out_weight,
):
    tensor_count = lax.axis_size("tensor")
    tensor_rank = lax.axis_index("tensor")
    requests = decode_queries.shape[1]
    groups = cache_keys.shape[1]
    reach = cache_keys.shape[2]
    model_width = decode_queries.shape[2]
    width = out_weight.shape[0]
    assert HEAD_DIM % width == 0
    factor = 1.0 / math.sqrt(HEAD_DIM)
    query_heads = decode_queries[0].reshape(requests, HEADS, HEAD_DIM)
    diagonal = jnp.arange(HEADS, dtype=jnp.int32)[:, None] == jnp.arange(HEADS, dtype=jnp.int32)[None, :]
    query_blocks = jnp.where(
        diagonal[None, :, :, None], query_heads[:, :, None, :], jnp.zeros((), query_heads.dtype)
    ).reshape(requests * HEADS, HEADS * HEAD_DIM)
    key_rows = cache_keys[0].reshape(groups * reach, HEADS * HEAD_DIM)
    value_rows = cache_values[0].reshape(groups * reach, HEADS * HEAD_DIM)
    scores = (
        lax.dot_general(
            query_blocks, key_rows, (((1,), (1,)), ((), ())), preferred_element_type=jnp.float32
        ).reshape(requests, HEADS, groups, reach)
        * factor
    )
    positions = tensor_rank * reach + jnp.arange(reach, dtype=jnp.int32)
    member = group_of[0][:, None] == jnp.arange(groups, dtype=jnp.int32)[None, :]
    within = positions[None, :] < cache_lengths[0][:, None]
    visible = (member[:, :, None] & within[None, :, :])[:, None, :, :]
    own_keys = new_keys[0].astype(jnp.float32).reshape(requests, HEADS, HEAD_DIM)
    own_score = jnp.sum(query_heads.astype(jnp.float32) * own_keys, axis=2) * factor
    local_peak = jnp.maximum(jnp.max(jnp.where(visible, scores, -jnp.inf), axis=(2, 3)), own_score)
    expon = jnp.where(visible, jnp.exp(scores - local_peak[:, :, None, None]), 0.0)
    probs = expon.astype(jnp.bfloat16).reshape(requests * HEADS, groups * reach)
    local_totals = jnp.sum(expon, axis=(2, 3))
    every_head = jnp.dot(probs, value_rows, preferred_element_type=jnp.float32).reshape(
        requests, HEADS, HEADS, HEAD_DIM
    )
    mixture = jnp.sum(
        jnp.where(diagonal[None, :, :, None], every_head, 0.0), axis=2
    ).reshape(requests, tensor_count, width)
    head_of = (jnp.arange(tensor_count, dtype=jnp.int32) * width) // HEAD_DIM
    peak_to = local_peak.T[head_of]
    totals_to = local_totals.T[head_of]
    flat_mix = jnp.transpose(mixture, (1, 0, 2)).reshape(tensor_count, requests * width)
    payload = jnp.concatenate([flat_mix, peak_to, totals_to], axis=1)
    received = lax.all_to_all(payload, "tensor", 0, 0, tiled=True)
    mixed_width = requests * width
    part_mix = received[:, :mixed_width].reshape(tensor_count, requests, width)
    part_peak = received[:, mixed_width:mixed_width + requests]
    part_totals = received[:, mixed_width + requests:]
    peak = jnp.max(part_peak, axis=0)
    scale = jnp.exp(part_peak - peak[None, :])
    my_head = (tensor_rank * width) // HEAD_DIM
    first_column = tensor_rank * width
    own_here = lax.dynamic_index_in_dim(own_score, my_head, axis=1, keepdims=False)
    own_exp = jnp.exp(own_here - peak)
    own_prob = lax.optimization_barrier(own_exp.astype(jnp.bfloat16)).astype(jnp.float32)
    totals = jnp.sum(scale * part_totals, axis=0) + own_exp
    own_values = lax.dynamic_slice_in_dim(new_values[0], first_column, width, 1).astype(jnp.float32)
    summed_mix = jnp.sum(scale[:, :, None] * part_mix, axis=0) + own_prob[:, None] * own_values
    attended = (summed_mix / totals[:, None]).astype(jnp.bfloat16)
    partial = jnp.dot(attended, out_weight, preferred_element_type=jnp.float32)
    per_device = requests // tensor_count
    gathered = lax.all_to_all(
        partial.reshape(tensor_count, per_device, model_width), "tensor", 0, 0, tiled=True
    )
    projected = jnp.sum(gathered, axis=0)
    return (decode_residual[0].astype(jnp.float32) + projected).astype(jnp.bfloat16)


def per_device(
    decode_queries,
    new_keys,
    new_values,
    cache_keys,
    cache_values,
    group_of,
    cache_lengths,
    decode_residual,
    out_weight,
    prefill_states,
    norm_gain,
    routes,
    route_weights,
    w_gate,
    w_up,
    w_down,
):
    tensor_count = lax.axis_size("tensor")
    model_width = decode_queries.shape[2]
    decode_hidden = attention_rows(
        decode_queries,
        new_keys,
        new_values,
        cache_keys,
        cache_values,
        group_of,
        cache_lengths,
        decode_residual,
        out_weight,
    )
    residual_rows = jnp.concatenate([prefill_states, decode_hidden], axis=0)
    row_float = residual_rows.astype(jnp.float32)
    inverse = lax.rsqrt(jnp.mean(row_float * row_float, axis=1, keepdims=True) + 1e-06)
    normed = (row_float * inverse * norm_gain).astype(jnp.bfloat16)
    row_count, top_count = routes.shape
    capacity = max(8, (row_count * top_count * 3 // (2 * tensor_count) + 7) // 8 * 8)
    flat_expert = routes.reshape(-1)
    one_hot = (flat_expert[:, None] == jnp.arange(tensor_count, dtype=jnp.int32)[None, :]).astype(
        jnp.int32
    )
    earlier = jnp.cumsum(one_hot, axis=0) - one_hot
    rank_within = jnp.sum(earlier * one_hot, axis=1)
    slot_index = flat_expert * capacity + rank_within
    slots = jnp.arange(tensor_count * capacity, dtype=jnp.int32)
    select = jnp.any(
        slot_index.reshape(row_count, top_count)[None, :, :] == slots[:, None, None], axis=2
    ).astype(jnp.bfloat16)
    outgoing = jnp.dot(select, normed, preferred_element_type=jnp.float32).astype(jnp.bfloat16)
    outgoing = outgoing.reshape(tensor_count, capacity, model_width)
    both_groups = lax.all_gather(
        lax.all_to_all(outgoing, "tensor", split_axis=0, concat_axis=0, tiled=True),
        "dp",
        axis=0,
        tiled=True,
    )
    block = both_groups
    returned = lax.all_to_all(
        lax.psum_scatter(
            expert_mlp(block, w_gate[0], w_up[0], w_down[0])
            .reshape(block.shape)
            .astype(jnp.bfloat16),
            "dp",
            scatter_dimension=0,
            tiled=True,
        ),
        "tensor",
        split_axis=0,
        concat_axis=0,
        tiled=True,
    )
    returned = returned.reshape(tensor_count * capacity, model_width)
    columns = jnp.arange(tensor_count * capacity, dtype=jnp.int32)
    mixing = jnp.sum(
        jnp.where(
            slot_index.reshape(row_count, top_count)[:, :, None] == columns[None, None, :],
            route_weights[:, :, None],
            0.0,
        ),
        axis=1,
    )
    high = mixing.astype(jnp.bfloat16)
    rest = mixing - high.astype(jnp.float32)
    middle = rest.astype(jnp.bfloat16)
    low = (rest - middle.astype(jnp.float32)).astype(jnp.bfloat16)
    prefill_count = prefill_states.shape[0]

    def combined(lo, hi):
        parts = jnp.dot(
            jnp.concatenate([high[lo:hi], middle[lo:hi], low[lo:hi]], axis=0),
            returned,
            preferred_element_type=jnp.float32,
        ).reshape(3, hi - lo, model_width)
        weighted = (parts[0] + parts[1]) + parts[2]
        return (row_float[lo:hi] + weighted).astype(jnp.bfloat16)

    return (combined(0, prefill_count), combined(prefill_count, row_count)[None])


def solution(mesh):
    in_specs = (
        P("dp", None, None),
        P("dp", None, None),
        P("dp", None, None),
        P("dp", None, "tensor", None),
        P("dp", None, "tensor", None),
        P("dp", None),
        P("dp", None),
        P("dp", "tensor", None),
        P("tensor", None),
        P(("dp", "tensor"), None),
        P(),
        P(("dp", "tensor"), None),
        P(("dp", "tensor"), None),
        P("tensor", None, "dp"),
        P("tensor", None, "dp"),
        P("tensor", "dp", None),
    )
    out_specs = (P(("dp", "tensor"), None), P("dp", "tensor", None))
    return jax.shard_map(
        per_device, mesh=mesh, in_specs=in_specs, out_specs=out_specs, check_vma=False
    )
```

```python
import math

import jax
import jax.numpy as jnp
from jax import lax
from jax.sharding import PartitionSpec as P

HEADS = 16
HEAD_DIM = 128


def expert_mlp(inputs, gate_w, up_w, down_w):
    flat_rows = inputs.reshape(-1, inputs.shape[-1])
    gate = jnp.dot(flat_rows, gate_w, preferred_element_type=jnp.float32)
    upper = jnp.dot(flat_rows, up_w, preferred_element_type=jnp.float32)
    active = (jax.nn.silu(gate) * upper).astype(jnp.bfloat16)
    return jnp.dot(active, down_w, preferred_element_type=jnp.float32)


def attention_partials(
    decode_queries, new_keys, cache_keys, cache_values, group_of, cache_lengths, width
):
    tensor_count = lax.axis_size("tensor")
    tensor_rank = lax.axis_index("tensor")
    requests = decode_queries.shape[1]
    groups = cache_keys.shape[1]
    reach = cache_keys.shape[2]
    model_width = decode_queries.shape[2]
    assert HEAD_DIM % width == 0
    factor = 1.0 / math.sqrt(HEAD_DIM)
    query_heads = decode_queries[0].reshape(requests, HEADS, HEAD_DIM)
    key_table = cache_keys[0].reshape(groups, reach, HEADS, HEAD_DIM)
    value_table = cache_values[0].reshape(groups, reach, HEADS, HEAD_DIM)
    scores = (
        jnp.einsum("rhd,gjhd->grhj", query_heads, key_table, preferred_element_type=jnp.float32)
        * factor
    )
    positions = tensor_rank * reach + jnp.arange(reach, dtype=jnp.int32)
    member = group_of[0][None, :] == jnp.arange(groups, dtype=jnp.int32)[:, None]
    within = positions[None, :] < cache_lengths[0][:, None]
    visible = (member[:, :, None] & within[:, None, :])[:, :, None, :]
    own_keys = new_keys[0].astype(jnp.float32).reshape(requests, HEADS, HEAD_DIM)
    own_score = jnp.sum(query_heads.astype(jnp.float32) * own_keys, axis=2) * factor
    local_peak = jnp.maximum(jnp.max(jnp.where(visible, scores, -jnp.inf), axis=(0, 3)), own_score)
    expon = jnp.where(visible, jnp.exp(scores - local_peak[None, :, :, None]), 0.0)
    probs = expon.astype(jnp.bfloat16)
    local_totals = jnp.sum(expon, axis=(0, 3))
    mixture = jnp.einsum(
        "grhj,gjhd->rhd", probs, value_table, preferred_element_type=jnp.float32
    ).reshape(requests, tensor_count, width)
    head_of = (jnp.arange(tensor_count, dtype=jnp.int32) * width) // HEAD_DIM
    peak_to = local_peak.T[head_of]
    totals_to = local_totals.T[head_of]
    flat_mix = jnp.transpose(mixture, (1, 0, 2)).reshape(tensor_count, requests * width)
    payload = jnp.concatenate([flat_mix, peak_to, totals_to], axis=1)
    return payload, own_score


def attention_finish(payload, own_score, new_values, decode_residual, out_weight):
    tensor_count = lax.axis_size("tensor")
    tensor_rank = lax.axis_index("tensor")
    requests, model_width = new_values.shape[1], new_values.shape[2]
    width = out_weight.shape[0]
    received = lax.all_to_all(payload, "tensor", 0, 0, tiled=True)
    mixed_width = requests * width
    part_mix = received[:, :mixed_width].reshape(tensor_count, requests, width)
    part_peak = received[:, mixed_width:mixed_width + requests]
    part_totals = received[:, mixed_width + requests:]
    peak = jnp.max(part_peak, axis=0)
    scale = jnp.exp(part_peak - peak[None, :])
    my_head = (tensor_rank * width) // HEAD_DIM
    first_column = tensor_rank * width
    own_here = lax.dynamic_index_in_dim(own_score, my_head, axis=1, keepdims=False)
    own_exp = jnp.exp(own_here - peak)
    own_prob = lax.optimization_barrier(own_exp.astype(jnp.bfloat16)).astype(jnp.float32)
    totals = jnp.sum(scale * part_totals, axis=0) + own_exp
    own_values = lax.dynamic_slice_in_dim(new_values[0], first_column, width, 1).astype(jnp.float32)
    summed_mix = jnp.sum(scale[:, :, None] * part_mix, axis=0) + own_prob[:, None] * own_values
    attended = (summed_mix / totals[:, None]).astype(jnp.bfloat16)
    partial = jnp.dot(attended, out_weight, preferred_element_type=jnp.float32)
    per_device = requests // tensor_count
    gathered = lax.all_to_all(
        partial.reshape(tensor_count, per_device, model_width), "tensor", 0, 0, tiled=True
    )
    projected = jnp.sum(gathered, axis=0)
    return (decode_residual[0].astype(jnp.float32) + projected).astype(jnp.bfloat16)


def rms_normed(residual_rows, norm_gain):
    row_float = residual_rows.astype(jnp.float32)
    inverse = lax.rsqrt(jnp.mean(row_float * row_float, axis=1, keepdims=True) + 1e-06)
    return row_float, (row_float * inverse * norm_gain).astype(jnp.bfloat16)


def dispatch(normed, slot_index, slot_count):
    row_count = normed.shape[0]
    slots = jnp.arange(slot_count, dtype=jnp.int32)
    select = jnp.any(
        slot_index.reshape(row_count, -1)[None, :, :] == slots[:, None, None], axis=2
    ).astype(jnp.bfloat16)
    outgoing = jnp.dot(select, normed, preferred_element_type=jnp.float32).astype(jnp.bfloat16)
    tensor_count = lax.axis_size("tensor")
    outgoing = outgoing.reshape(tensor_count, slot_count // tensor_count, normed.shape[1])
    return lax.all_to_all(outgoing, "tensor", split_axis=0, concat_axis=0, tiled=True)


def experts_on(received, experts):
    block = lax.all_gather(received, "dp", axis=0, tiled=True)
    return expert_mlp(block, *experts).reshape(block.shape).astype(jnp.bfloat16)


def rank_in_expert(flat_expert, tensor_count):
    one_hot = (flat_expert[:, None] == jnp.arange(tensor_count, dtype=jnp.int32)[None, :]).astype(
        jnp.int32
    )
    earlier = jnp.cumsum(one_hot, axis=0) - one_hot
    return jnp.sum(earlier * one_hot, axis=1), jnp.sum(one_hot, axis=0)


def per_device(
    decode_queries,
    new_keys,
    new_values,
    cache_keys,
    cache_values,
    group_of,
    cache_lengths,
    decode_residual,
    out_weight,
    prefill_states,
    norm_gain,
    routes,
    route_weights,
    w_gate,
    w_up,
    w_down,
):
    tensor_count = lax.axis_size("tensor")
    model_width = decode_queries.shape[2]
    prefill_count = prefill_states.shape[0]
    row_count, top_count = routes.shape
    decode_count = row_count - prefill_count
    capacity = max(8, (row_count * top_count * 3 // (2 * tensor_count) + 7) // 8 * 8)
    early = max(8, capacity * 2 // 3 // 8 * 8)
    late = max(capacity - early, decode_count)
    stride = early + late
    experts = (w_gate[0], w_up[0], w_down[0])
    prefill_routes = routes[:prefill_count].reshape(-1)
    decode_routes = routes[prefill_count:].reshape(-1)
    prefill_rank, prefill_counts = rank_in_expert(prefill_routes, tensor_count)
    decode_rank, _ = rank_in_expert(decode_routes, tensor_count)
    overflow = jnp.maximum(prefill_counts - early, 0)
    prefill_float, prefill_normed = rms_normed(prefill_states, norm_gain)
    first_in = dispatch(
        prefill_normed,
        jnp.where(prefill_rank < early, prefill_routes * early + prefill_rank, -1),
        tensor_count * early,
    )
    payload, own_score = attention_partials(
        decode_queries, new_keys, cache_keys, cache_values, group_of, cache_lengths,
        out_weight.shape[0],
    )
    payload, first_in = lax.optimization_barrier((payload, first_in))
    first_done = experts_on(first_in, experts)
    decode_hidden = attention_finish(payload, own_score, new_values, decode_residual, out_weight)
    decode_float, decode_normed = rms_normed(decode_hidden, norm_gain)
    late_slot = jnp.concatenate(
        [
            jnp.where(
                prefill_rank >= early, prefill_routes * late + prefill_rank - early, -1
            ),
            decode_routes * late + overflow[decode_routes] + decode_rank,
        ]
    )
    second_in = dispatch(
        jnp.concatenate([prefill_normed, decode_normed], axis=0), late_slot, tensor_count * late
    )
    second_done = experts_on(second_in, experts)
    merged = jnp.concatenate([first_done, second_done], axis=1)
    returned = lax.all_to_all(
        lax.psum_scatter(merged, "dp", scatter_dimension=0, tiled=True),
        "tensor",
        split_axis=0,
        concat_axis=0,
        tiled=True,
    ).reshape(tensor_count * stride, model_width)
    place = jnp.concatenate(
        [
            prefill_routes * stride + prefill_rank,
            decode_routes * stride + early + overflow[decode_routes] + decode_rank,
        ]
    ).reshape(row_count, top_count)
    columns = jnp.arange(tensor_count * stride, dtype=jnp.int32)
    mixing = jnp.sum(
        jnp.where(place[:, :, None] == columns[None, None, :], route_weights[:, :, None], 0.0),
        axis=1,
    )
    high = mixing.astype(jnp.bfloat16)
    rest = mixing - high.astype(jnp.float32)
    middle = rest.astype(jnp.bfloat16)
    low = (rest - middle.astype(jnp.float32)).astype(jnp.bfloat16)

    def combined(lo, hi, row_float):
        parts = jnp.dot(
            jnp.concatenate([high[lo:hi], middle[lo:hi], low[lo:hi]], axis=0),
            returned,
            preferred_element_type=jnp.float32,
        ).reshape(3, hi - lo, model_width)
        weighted = (parts[0] + parts[1]) + parts[2]
        return (row_float + weighted).astype(jnp.bfloat16)

    return (
        combined(0, prefill_count, prefill_float),
        combined(prefill_count, row_count, decode_float)[None],
    )


def solution(mesh):
    in_specs = (
        P("dp", None, None),
        P("dp", None, None),
        P("dp", None, None),
        P("dp", None, "tensor", None),
        P("dp", None, "tensor", None),
        P("dp", None),
        P("dp", None),
        P("dp", "tensor", None),
        P("tensor", None),
        P(("dp", "tensor"), None),
        P(),
        P(("dp", "tensor"), None),
        P(("dp", "tensor"), None),
        P("tensor", None, "dp"),
        P("tensor", None, "dp"),
        P("tensor", "dp", None),
    )
    out_specs = (P(("dp", "tensor"), None), P("dp", "tensor", None))
    return jax.shard_map(
        per_device, mesh=mesh, in_specs=in_specs, out_specs=out_specs, check_vma=False
    )
```

```python
import math

import jax
import jax.numpy as jnp
from jax import lax
from jax.sharding import PartitionSpec as P

HEADS = 16
HEAD_DIM = 128


def expert_mlp(inputs, gate_w, up_w, down_w):
    flat_rows = inputs.reshape(-1, inputs.shape[-1])
    gate = jnp.dot(flat_rows, gate_w, preferred_element_type=jnp.float32)
    upper = jnp.dot(flat_rows, up_w, preferred_element_type=jnp.float32)
    active = (jax.nn.silu(gate) * upper).astype(jnp.bfloat16)
    return jnp.dot(active, down_w, preferred_element_type=jnp.float32)


def attention_partials(
    decode_queries, new_keys, cache_keys, cache_values, group_of, cache_lengths, width
):
    tensor_count = lax.axis_size("tensor")
    tensor_rank = lax.axis_index("tensor")
    requests = decode_queries.shape[1]
    groups = cache_keys.shape[1]
    reach = cache_keys.shape[2]
    model_width = decode_queries.shape[2]
    assert HEAD_DIM % width == 0
    factor = 1.0 / math.sqrt(HEAD_DIM)
    query_heads = decode_queries[0].reshape(requests, HEADS, HEAD_DIM)
    key_table = cache_keys[0].reshape(groups, reach, HEADS, HEAD_DIM)
    value_table = cache_values[0].reshape(groups, reach, HEADS, HEAD_DIM)
    scores = (
        jnp.einsum("rhd,gjhd->grhj", query_heads, key_table, preferred_element_type=jnp.float32)
        * factor
    )
    positions = tensor_rank * reach + jnp.arange(reach, dtype=jnp.int32)
    member = group_of[0][None, :] == jnp.arange(groups, dtype=jnp.int32)[:, None]
    within = positions[None, :] < cache_lengths[0][:, None]
    visible = (member[:, :, None] & within[:, None, :])[:, :, None, :]
    own_keys = new_keys[0].astype(jnp.float32).reshape(requests, HEADS, HEAD_DIM)
    own_score = jnp.sum(query_heads.astype(jnp.float32) * own_keys, axis=2) * factor
    local_peak = jnp.maximum(jnp.max(jnp.where(visible, scores, -jnp.inf), axis=(0, 3)), own_score)
    expon = jnp.where(visible, jnp.exp(scores - local_peak[None, :, :, None]), 0.0)
    probs = expon.astype(jnp.bfloat16)
    local_totals = jnp.sum(expon, axis=(0, 3))
    mixture = jnp.einsum(
        "grhj,gjhd->rhd", probs, value_table, preferred_element_type=jnp.float32
    ).reshape(requests, tensor_count, width)
    head_of = (jnp.arange(tensor_count, dtype=jnp.int32) * width) // HEAD_DIM
    peak_to = local_peak.T[head_of]
    totals_to = local_totals.T[head_of]
    flat_mix = jnp.transpose(mixture, (1, 0, 2)).reshape(tensor_count, requests * width)
    payload = jnp.concatenate([flat_mix, peak_to, totals_to], axis=1)
    return payload, own_score


def attention_finish(payload, own_score, new_values, decode_residual, out_weight):
    tensor_count = lax.axis_size("tensor")
    tensor_rank = lax.axis_index("tensor")
    requests, model_width = new_values.shape[1], new_values.shape[2]
    width = out_weight.shape[0]
    received = lax.all_to_all(payload, "tensor", 0, 0, tiled=True)
    mixed_width = requests * width
    part_mix = received[:, :mixed_width].reshape(tensor_count, requests, width)
    part_peak = received[:, mixed_width:mixed_width + requests]
    part_totals = received[:, mixed_width + requests:]
    peak = jnp.max(part_peak, axis=0)
    scale = jnp.exp(part_peak - peak[None, :])
    my_head = (tensor_rank * width) // HEAD_DIM
    first_column = tensor_rank * width
    own_here = lax.dynamic_index_in_dim(own_score, my_head, axis=1, keepdims=False)
    own_exp = jnp.exp(own_here - peak)
    own_prob = lax.optimization_barrier(own_exp.astype(jnp.bfloat16)).astype(jnp.float32)
    totals = jnp.sum(scale * part_totals, axis=0) + own_exp
    own_values = lax.dynamic_slice_in_dim(new_values[0], first_column, width, 1).astype(jnp.float32)
    summed_mix = jnp.sum(scale[:, :, None] * part_mix, axis=0) + own_prob[:, None] * own_values
    attended = (summed_mix / totals[:, None]).astype(jnp.bfloat16)
    partial = jnp.dot(attended, out_weight, preferred_element_type=jnp.float32)
    per_device = requests // tensor_count
    gathered = lax.all_to_all(
        partial.reshape(tensor_count, per_device, model_width), "tensor", 0, 0, tiled=True
    )
    projected = jnp.sum(gathered, axis=0)
    return (decode_residual[0].astype(jnp.float32) + projected).astype(jnp.bfloat16)


def rms_normed(residual_rows, norm_gain):
    row_float = residual_rows.astype(jnp.float32)
    inverse = lax.rsqrt(jnp.mean(row_float * row_float, axis=1, keepdims=True) + 1e-06)
    return row_float, (row_float * inverse * norm_gain).astype(jnp.bfloat16)


def dispatch(normed, slot_index, slot_count):
    row_count = normed.shape[0]
    slots = jnp.arange(slot_count, dtype=jnp.int32)
    select = jnp.any(
        slot_index.reshape(row_count, -1)[None, :, :] == slots[:, None, None], axis=2
    ).astype(jnp.bfloat16)
    outgoing = jnp.dot(select, normed, preferred_element_type=jnp.float32).astype(jnp.bfloat16)
    tensor_count = lax.axis_size("tensor")
    outgoing = outgoing.reshape(tensor_count, slot_count // tensor_count, normed.shape[1])
    return lax.all_to_all(outgoing, "tensor", split_axis=0, concat_axis=0, tiled=True)


def experts_on(received, experts):
    block = lax.all_gather(received, "dp", axis=0, tiled=True)
    return expert_mlp(block, *experts).reshape(block.shape).astype(jnp.bfloat16)


def rank_in_expert(flat_expert, tensor_count):
    one_hot = (flat_expert[:, None] == jnp.arange(tensor_count, dtype=jnp.int32)[None, :]).astype(
        jnp.int32
    )
    earlier = jnp.cumsum(one_hot, axis=0) - one_hot
    return jnp.sum(earlier * one_hot, axis=1), jnp.sum(one_hot, axis=0)


def give_back(done):
    return lax.all_to_all(
        lax.psum_scatter(done, "dp", scatter_dimension=0, tiled=True),
        "tensor",
        split_axis=0,
        concat_axis=0,
        tiled=True,
    )


def per_device(
    decode_queries,
    new_keys,
    new_values,
    cache_keys,
    cache_values,
    group_of,
    cache_lengths,
    decode_residual,
    out_weight,
    prefill_states,
    norm_gain,
    routes,
    route_weights,
    w_gate,
    w_up,
    w_down,
):
    tensor_count = lax.axis_size("tensor")
    model_width = decode_queries.shape[2]
    prefill_count = prefill_states.shape[0]
    row_count, top_count = routes.shape
    decode_count = row_count - prefill_count
    capacity = max(8, (row_count * top_count * 3 // (2 * tensor_count) + 7) // 8 * 8)
    early = max(8, capacity * 2 // 3 // 8 * 8)
    late = max(capacity - early, decode_count)
    stride = early + late
    experts = (w_gate[0], w_up[0], w_down[0])
    prefill_routes = routes[:prefill_count].reshape(-1)
    decode_routes = routes[prefill_count:].reshape(-1)
    prefill_rank, prefill_counts = rank_in_expert(prefill_routes, tensor_count)
    decode_rank, _ = rank_in_expert(decode_routes, tensor_count)
    overflow = jnp.maximum(prefill_counts - early, 0)
    prefill_float, prefill_normed = rms_normed(prefill_states, norm_gain)
    first_in = dispatch(
        prefill_normed,
        jnp.where(prefill_rank < early, prefill_routes * early + prefill_rank, -1),
        tensor_count * early,
    )
    payload, own_score = attention_partials(
        decode_queries, new_keys, cache_keys, cache_values, group_of, cache_lengths,
        out_weight.shape[0],
    )
    payload, first_in = lax.optimization_barrier((payload, first_in))
    first_done = experts_on(first_in, experts)
    decode_hidden = attention_finish(payload, own_score, new_values, decode_residual, out_weight)
    decode_float, decode_normed = rms_normed(decode_hidden, norm_gain)
    late_slot = jnp.concatenate(
        [
            jnp.where(
                prefill_rank >= early, prefill_routes * late + prefill_rank - early, -1
            ),
            decode_routes * late + overflow[decode_routes] + decode_rank,
        ]
    )
    second_in = dispatch(
        jnp.concatenate([prefill_normed, decode_normed], axis=0), late_slot, tensor_count * late
    )
    first_done, second_in = lax.optimization_barrier((first_done, second_in))
    first_back = give_back(first_done)
    second_done = experts_on(second_in, experts)
    first_back, second_done = lax.optimization_barrier((first_back, second_done))
    second_back = give_back(second_done)
    returned = jnp.concatenate([first_back, second_back], axis=1).reshape(
        tensor_count * stride, model_width
    )
    place = jnp.concatenate(
        [
            prefill_routes * stride + prefill_rank,
            decode_routes * stride + early + overflow[decode_routes] + decode_rank,
        ]
    ).reshape(row_count, top_count)
    columns = jnp.arange(tensor_count * stride, dtype=jnp.int32)
    mixing = jnp.sum(
        jnp.where(place[:, :, None] == columns[None, None, :], route_weights[:, :, None], 0.0),
        axis=1,
    )
    high = mixing.astype(jnp.bfloat16)
    rest = mixing - high.astype(jnp.float32)
    middle = rest.astype(jnp.bfloat16)
    low = (rest - middle.astype(jnp.float32)).astype(jnp.bfloat16)

    def combined(lo, hi, row_float):
        parts = jnp.dot(
            jnp.concatenate([high[lo:hi], middle[lo:hi], low[lo:hi]], axis=0),
            returned,
            preferred_element_type=jnp.float32,
        ).reshape(3, hi - lo, model_width)
        weighted = (parts[0] + parts[1]) + parts[2]
        return (row_float + weighted).astype(jnp.bfloat16)

    return (
        combined(0, prefill_count, prefill_float),
        combined(prefill_count, row_count, decode_float)[None],
    )


def solution(mesh):
    in_specs = (
        P("dp", None, None),
        P("dp", None, None),
        P("dp", None, None),
        P("dp", None, "tensor", None),
        P("dp", None, "tensor", None),
        P("dp", None),
        P("dp", None),
        P("dp", "tensor", None),
        P("tensor", None),
        P(("dp", "tensor"), None),
        P(),
        P(("dp", "tensor"), None),
        P(("dp", "tensor"), None),
        P("tensor", None, "dp"),
        P("tensor", None, "dp"),
        P("tensor", "dp", None),
    )
    out_specs = (P(("dp", "tensor"), None), P("dp", "tensor", None))
    return jax.shard_map(
        per_device, mesh=mesh, in_specs=in_specs, out_specs=out_specs, check_vma=False
    )
```

```python
import math

import jax
import jax.numpy as jnp
from jax import lax
from jax.sharding import PartitionSpec as P

HEADS = 16
HEAD_DIM = 128


def expert_mlp(inputs, gate_w, up_w, down_w):
    flat_rows = inputs.reshape(-1, inputs.shape[-1])
    gate = jnp.dot(flat_rows, gate_w, preferred_element_type=jnp.float32)
    upper = jnp.dot(flat_rows, up_w, preferred_element_type=jnp.float32)
    active = (jax.nn.silu(gate) * upper).astype(jnp.bfloat16)
    return jnp.dot(active, down_w, preferred_element_type=jnp.float32)


def attention_partials(
    decode_queries, new_keys, cache_keys, cache_values, group_of, cache_lengths, width
):
    tensor_count = lax.axis_size("tensor")
    tensor_rank = lax.axis_index("tensor")
    requests = decode_queries.shape[1]
    groups = cache_keys.shape[1]
    reach = cache_keys.shape[2]
    model_width = decode_queries.shape[2]
    assert HEAD_DIM % width == 0
    factor = 1.0 / math.sqrt(HEAD_DIM)
    query_heads = decode_queries[0].reshape(requests, HEADS, HEAD_DIM)
    key_table = cache_keys[0].reshape(groups, reach, HEADS, HEAD_DIM)
    value_table = cache_values[0].reshape(groups, reach, HEADS, HEAD_DIM)
    scores = (
        jnp.einsum("rhd,gjhd->grhj", query_heads, key_table, preferred_element_type=jnp.float32)
        * factor
    )
    positions = tensor_rank * reach + jnp.arange(reach, dtype=jnp.int32)
    member = group_of[0][None, :] == jnp.arange(groups, dtype=jnp.int32)[:, None]
    within = positions[None, :] < cache_lengths[0][:, None]
    visible = (member[:, :, None] & within[:, None, :])[:, :, None, :]
    own_keys = new_keys[0].astype(jnp.float32).reshape(requests, HEADS, HEAD_DIM)
    own_score = jnp.sum(query_heads.astype(jnp.float32) * own_keys, axis=2) * factor
    local_peak = jnp.maximum(jnp.max(jnp.where(visible, scores, -jnp.inf), axis=(0, 3)), own_score)
    expon = jnp.where(visible, jnp.exp(scores - local_peak[None, :, :, None]), 0.0)
    probs = expon.astype(jnp.bfloat16)
    local_totals = jnp.sum(expon, axis=(0, 3))
    mixture = jnp.einsum(
        "grhj,gjhd->rhd", probs, value_table, preferred_element_type=jnp.float32
    ).reshape(requests, tensor_count, width)
    head_of = (jnp.arange(tensor_count, dtype=jnp.int32) * width) // HEAD_DIM
    peak_to = local_peak.T[head_of]
    totals_to = local_totals.T[head_of]
    flat_mix = jnp.transpose(mixture, (1, 0, 2)).reshape(tensor_count, requests * width)
    payload = jnp.concatenate([flat_mix, peak_to, totals_to], axis=1)
    return payload, own_score


def attention_finish(payload, own_score, new_values, decode_residual, out_weight):
    tensor_count = lax.axis_size("tensor")
    tensor_rank = lax.axis_index("tensor")
    requests, model_width = new_values.shape[1], new_values.shape[2]
    width = out_weight.shape[0]
    received = lax.all_to_all(payload, "tensor", 0, 0, tiled=True)
    mixed_width = requests * width
    part_mix = received[:, :mixed_width].reshape(tensor_count, requests, width)
    part_peak = received[:, mixed_width:mixed_width + requests]
    part_totals = received[:, mixed_width + requests:]
    peak = jnp.max(part_peak, axis=0)
    scale = jnp.exp(part_peak - peak[None, :])
    my_head = (tensor_rank * width) // HEAD_DIM
    first_column = tensor_rank * width
    own_here = lax.dynamic_index_in_dim(own_score, my_head, axis=1, keepdims=False)
    own_exp = jnp.exp(own_here - peak)
    own_prob = lax.optimization_barrier(own_exp.astype(jnp.bfloat16)).astype(jnp.float32)
    totals = jnp.sum(scale * part_totals, axis=0) + own_exp
    own_values = lax.dynamic_slice_in_dim(new_values[0], first_column, width, 1).astype(jnp.float32)
    summed_mix = jnp.sum(scale[:, :, None] * part_mix, axis=0) + own_prob[:, None] * own_values
    attended = (summed_mix / totals[:, None]).astype(jnp.bfloat16)
    partial = jnp.dot(attended, out_weight, preferred_element_type=jnp.float32)
    per_device = requests // tensor_count
    gathered = lax.all_to_all(
        partial.reshape(tensor_count, per_device, model_width), "tensor", 0, 0, tiled=True
    )
    projected = jnp.sum(gathered, axis=0)
    return (decode_residual[0].astype(jnp.float32) + projected).astype(jnp.bfloat16)


def rms_normed(residual_rows, norm_gain):
    row_float = residual_rows.astype(jnp.float32)
    inverse = lax.rsqrt(jnp.mean(row_float * row_float, axis=1, keepdims=True) + 1e-06)
    return row_float, (row_float * inverse * norm_gain).astype(jnp.bfloat16)


def dispatch(normed, slot_index, slot_count):
    row_count = normed.shape[0]
    slots = jnp.arange(slot_count, dtype=jnp.int32)
    select = jnp.any(
        slot_index.reshape(row_count, -1)[None, :, :] == slots[:, None, None], axis=2
    ).astype(jnp.bfloat16)
    outgoing = jnp.dot(select, normed, preferred_element_type=jnp.float32).astype(jnp.bfloat16)
    tensor_count = lax.axis_size("tensor")
    outgoing = outgoing.reshape(tensor_count, slot_count // tensor_count, normed.shape[1])
    return lax.all_to_all(outgoing, "tensor", split_axis=0, concat_axis=0, tiled=True)


def experts_on(received, experts):
    block = lax.all_gather(received, "dp", axis=0, tiled=True)
    return expert_mlp(block, *experts).reshape(block.shape).astype(jnp.bfloat16)


def rank_in_expert(flat_expert, tensor_count):
    one_hot = (flat_expert[:, None] == jnp.arange(tensor_count, dtype=jnp.int32)[None, :]).astype(
        jnp.int32
    )
    earlier = jnp.cumsum(one_hot, axis=0) - one_hot
    return jnp.sum(earlier * one_hot, axis=1), jnp.sum(one_hot, axis=0)


def give_back(done):
    return lax.all_to_all(
        lax.psum_scatter(done, "dp", scatter_dimension=0, tiled=True),
        "tensor",
        split_axis=0,
        concat_axis=0,
        tiled=True,
    )


def per_device(
    decode_queries,
    new_keys,
    new_values,
    cache_keys,
    cache_values,
    group_of,
    cache_lengths,
    decode_residual,
    out_weight,
    prefill_states,
    norm_gain,
    routes,
    route_weights,
    w_gate,
    w_up,
    w_down,
):
    tensor_count = lax.axis_size("tensor")
    model_width = decode_queries.shape[2]
    prefill_count = prefill_states.shape[0]
    row_count, top_count = routes.shape
    decode_count = row_count - prefill_count
    capacity = max(8, (row_count * top_count * 3 // (2 * tensor_count) + 7) // 8 * 8)
    early = max(8, capacity * 2 // 3 // 8 * 8)
    late = max(capacity - early, decode_count)
    stride = early + late
    experts = (w_gate[0], w_up[0], w_down[0])
    prefill_routes = routes[:prefill_count].reshape(-1)
    decode_routes = routes[prefill_count:].reshape(-1)
    prefill_rank, prefill_counts = rank_in_expert(prefill_routes, tensor_count)
    decode_rank, _ = rank_in_expert(decode_routes, tensor_count)
    overflow = jnp.maximum(prefill_counts - early, 0)
    prefill_float, prefill_normed = rms_normed(prefill_states, norm_gain)
    first_in = dispatch(
        prefill_normed,
        jnp.where(prefill_rank < early, prefill_routes * early + prefill_rank, -1),
        tensor_count * early,
    )
    payload, own_score = attention_partials(
        decode_queries, new_keys, cache_keys, cache_values, group_of, cache_lengths,
        out_weight.shape[0],
    )
    payload, first_in = lax.optimization_barrier((payload, first_in))
    first_done = experts_on(first_in, experts)
    decode_hidden = attention_finish(payload, own_score, new_values, decode_residual, out_weight)
    decode_float, decode_normed = rms_normed(decode_hidden, norm_gain)
    late_slot = jnp.concatenate(
        [
            jnp.where(
                prefill_rank >= early, prefill_routes * late + prefill_rank - early, -1
            ),
            decode_routes * late + overflow[decode_routes] + decode_rank,
        ]
    )
    second_in = dispatch(
        jnp.concatenate([prefill_normed, decode_normed], axis=0), late_slot, tensor_count * late
    )
    first_done, second_in = lax.optimization_barrier((first_done, second_in))
    first_back = give_back(first_done)
    second_done = experts_on(second_in, experts)
    first_back, second_done = lax.optimization_barrier((first_back, second_done))
    second_back = give_back(second_done)
    first_back = first_back.reshape(tensor_count * early, model_width)
    second_back = second_back.reshape(tensor_count * late, model_width)
    place = jnp.concatenate(
        [
            prefill_routes * stride + prefill_rank,
            decode_routes * stride + early + overflow[decode_routes] + decode_rank,
        ]
    ).reshape(row_count, top_count)
    columns = jnp.arange(tensor_count * stride, dtype=jnp.int32)
    mixing = jnp.sum(
        jnp.where(place[:, :, None] == columns[None, None, :], route_weights[:, :, None], 0.0),
        axis=1,
    )
    high = mixing.astype(jnp.bfloat16)
    rest = mixing - high.astype(jnp.float32)
    middle = rest.astype(jnp.bfloat16)
    low = (rest - middle.astype(jnp.float32)).astype(jnp.bfloat16)
    split = jnp.concatenate([high, middle, low], axis=0).reshape(3 * row_count, tensor_count, stride)
    first_mix = split[:, :, :early].reshape(3 * row_count, tensor_count * early)
    second_mix = split[:, :, early:].reshape(3 * row_count, tensor_count * late)
    first_sum = jnp.dot(first_mix, first_back, preferred_element_type=jnp.float32)
    second_sum = jnp.dot(second_mix, second_back, preferred_element_type=jnp.float32)
    parts = (first_sum + second_sum).reshape(3, row_count, model_width)
    weighted = (parts[0] + parts[1]) + parts[2]
    row_float = jnp.concatenate([prefill_float, decode_float], axis=0)
    mixed_rows = (row_float + weighted).astype(jnp.bfloat16)
    return (mixed_rows[:prefill_count], mixed_rows[prefill_count:][None])


def solution(mesh):
    in_specs = (
        P("dp", None, None),
        P("dp", None, None),
        P("dp", None, None),
        P("dp", None, "tensor", None),
        P("dp", None, "tensor", None),
        P("dp", None),
        P("dp", None),
        P("dp", "tensor", None),
        P("tensor", None),
        P(("dp", "tensor"), None),
        P(),
        P(("dp", "tensor"), None),
        P(("dp", "tensor"), None),
        P("tensor", None, "dp"),
        P("tensor", None, "dp"),
        P("tensor", "dp", None),
    )
    out_specs = (P(("dp", "tensor"), None), P("dp", "tensor", None))
    return jax.shard_map(
        per_device, mesh=mesh, in_specs=in_specs, out_specs=out_specs, check_vma=False
    )
```

```python
import math

import jax
import jax.numpy as jnp
from jax import lax
from jax.sharding import PartitionSpec as P

HEADS = 16
HEAD_DIM = 128


def expert_mlp(inputs, gate_w, up_w, down_w):
    flat_rows = inputs.reshape(-1, inputs.shape[-1])
    gate = jnp.dot(flat_rows, gate_w, preferred_element_type=jnp.float32)
    upper = jnp.dot(flat_rows, up_w, preferred_element_type=jnp.float32)
    active = (jax.nn.silu(gate) * upper).astype(jnp.bfloat16)
    return jnp.dot(active, down_w, preferred_element_type=jnp.float32)


def attention_partials(
    decode_queries, new_keys, cache_keys, cache_values, group_of, cache_lengths, width
):
    tensor_count = lax.axis_size("tensor")
    tensor_rank = lax.axis_index("tensor")
    requests = decode_queries.shape[1]
    groups = cache_keys.shape[1]
    reach = cache_keys.shape[2]
    model_width = decode_queries.shape[2]
    assert HEAD_DIM % width == 0
    factor = 1.0 / math.sqrt(HEAD_DIM)
    query_heads = decode_queries[0].reshape(requests, HEADS, HEAD_DIM)
    key_table = cache_keys[0].reshape(groups, reach, HEADS, HEAD_DIM)
    value_table = cache_values[0].reshape(groups, reach, HEADS, HEAD_DIM)
    scores = (
        jnp.einsum("rhd,gjhd->grhj", query_heads, key_table, preferred_element_type=jnp.float32)
        * factor
    )
    positions = tensor_rank * reach + jnp.arange(reach, dtype=jnp.int32)
    member = group_of[0][None, :] == jnp.arange(groups, dtype=jnp.int32)[:, None]
    within = positions[None, :] < cache_lengths[0][:, None]
    visible = (member[:, :, None] & within[:, None, :])[:, :, None, :]
    own_keys = new_keys[0].astype(jnp.float32).reshape(requests, HEADS, HEAD_DIM)
    own_score = jnp.sum(query_heads.astype(jnp.float32) * own_keys, axis=2) * factor
    local_peak = jnp.maximum(jnp.max(jnp.where(visible, scores, -jnp.inf), axis=(0, 3)), own_score)
    expon = jnp.where(visible, jnp.exp(scores - local_peak[None, :, :, None]), 0.0)
    probs = expon.astype(jnp.bfloat16)
    local_totals = jnp.sum(expon, axis=(0, 3))
    mixture = jnp.einsum(
        "grhj,gjhd->rhd", probs, value_table, preferred_element_type=jnp.float32
    ).reshape(requests, tensor_count, width)
    head_of = (jnp.arange(tensor_count, dtype=jnp.int32) * width) // HEAD_DIM
    peak_to = local_peak.T[head_of]
    totals_to = local_totals.T[head_of]
    flat_mix = jnp.transpose(mixture, (1, 0, 2)).reshape(tensor_count, requests * width)
    payload = jnp.concatenate([flat_mix, peak_to, totals_to], axis=1)
    return payload, own_score


def attention_finish(payload, own_score, new_values, decode_residual, out_weight):
    tensor_count = lax.axis_size("tensor")
    tensor_rank = lax.axis_index("tensor")
    requests, model_width = new_values.shape[1], new_values.shape[2]
    width = out_weight.shape[0]
    received = lax.all_to_all(payload, "tensor", 0, 0, tiled=True)
    mixed_width = requests * width
    part_mix = received[:, :mixed_width].reshape(tensor_count, requests, width)
    part_peak = received[:, mixed_width:mixed_width + requests]
    part_totals = received[:, mixed_width + requests:]
    peak = jnp.max(part_peak, axis=0)
    scale = jnp.exp(part_peak - peak[None, :])
    my_head = (tensor_rank * width) // HEAD_DIM
    first_column = tensor_rank * width
    own_here = lax.dynamic_index_in_dim(own_score, my_head, axis=1, keepdims=False)
    own_exp = jnp.exp(own_here - peak)
    own_prob = lax.optimization_barrier(own_exp.astype(jnp.bfloat16)).astype(jnp.float32)
    totals = jnp.sum(scale * part_totals, axis=0) + own_exp
    own_values = lax.dynamic_slice_in_dim(new_values[0], first_column, width, 1).astype(jnp.float32)
    summed_mix = jnp.sum(scale[:, :, None] * part_mix, axis=0) + own_prob[:, None] * own_values
    attended = (summed_mix / totals[:, None]).astype(jnp.bfloat16)
    partial = jnp.dot(attended, out_weight, preferred_element_type=jnp.float32)
    per_device = requests // tensor_count
    gathered = lax.all_to_all(
        partial.astype(jnp.bfloat16).reshape(tensor_count, per_device, model_width),
        "tensor", 0, 0, tiled=True,
    )
    projected = jnp.sum(gathered.astype(jnp.float32), axis=0)
    return (decode_residual[0].astype(jnp.float32) + projected).astype(jnp.bfloat16)


def rms_normed(residual_rows, norm_gain):
    row_float = residual_rows.astype(jnp.float32)
    inverse = lax.rsqrt(jnp.mean(row_float * row_float, axis=1, keepdims=True) + 1e-06)
    return row_float, (row_float * inverse * norm_gain).astype(jnp.bfloat16)


def dispatch(normed, slot_index, slot_count):
    row_count = normed.shape[0]
    slots = jnp.arange(slot_count, dtype=jnp.int32)
    select = jnp.any(
        slot_index.reshape(row_count, -1)[None, :, :] == slots[:, None, None], axis=2
    ).astype(jnp.bfloat16)
    outgoing = jnp.dot(select, normed, preferred_element_type=jnp.float32).astype(jnp.bfloat16)
    tensor_count = lax.axis_size("tensor")
    outgoing = outgoing.reshape(tensor_count, slot_count // tensor_count, normed.shape[1])
    return lax.all_to_all(outgoing, "tensor", split_axis=0, concat_axis=0, tiled=True)


def experts_on(received, experts):
    block = lax.all_gather(received, "dp", axis=0, tiled=True)
    return expert_mlp(block, *experts).reshape(block.shape).astype(jnp.bfloat16)


def rank_in_expert(flat_expert, tensor_count):
    one_hot = (flat_expert[:, None] == jnp.arange(tensor_count, dtype=jnp.int32)[None, :]).astype(
        jnp.int32
    )
    count = flat_expert.shape[0]
    lower = (
        jnp.arange(count, dtype=jnp.int32)[:, None] > jnp.arange(count, dtype=jnp.int32)[None, :]
    ).astype(jnp.bfloat16)
    earlier = jnp.dot(
        lower, one_hot.astype(jnp.bfloat16), preferred_element_type=jnp.float32
    ).astype(jnp.int32)
    return jnp.sum(earlier * one_hot, axis=1), jnp.sum(one_hot, axis=0)


def give_back(done):
    return lax.all_to_all(
        lax.psum_scatter(done, "dp", scatter_dimension=0, tiled=True),
        "tensor",
        split_axis=0,
        concat_axis=0,
        tiled=True,
    )


def per_device(
    decode_queries,
    new_keys,
    new_values,
    cache_keys,
    cache_values,
    group_of,
    cache_lengths,
    decode_residual,
    out_weight,
    prefill_states,
    norm_gain,
    routes,
    route_weights,
    w_gate,
    w_up,
    w_down,
):
    tensor_count = lax.axis_size("tensor")
    model_width = decode_queries.shape[2]
    prefill_count = prefill_states.shape[0]
    row_count, top_count = routes.shape
    decode_count = row_count - prefill_count
    capacity = max(8, (row_count * top_count * 3 // (2 * tensor_count) + 7) // 8 * 8)
    early = max(8, capacity * 2 // 3 // 8 * 8)
    late = max(capacity - early, decode_count)
    stride = early + late
    experts = (w_gate[0], w_up[0], w_down[0])
    prefill_routes = routes[:prefill_count].reshape(-1)
    decode_routes = routes[prefill_count:].reshape(-1)
    prefill_rank, prefill_counts = rank_in_expert(prefill_routes, tensor_count)
    decode_rank, _ = rank_in_expert(decode_routes, tensor_count)
    overflow = jnp.maximum(prefill_counts - early, 0)
    prefill_float, prefill_normed = rms_normed(prefill_states, norm_gain)
    first_in = dispatch(
        prefill_normed,
        jnp.where(prefill_rank < early, prefill_routes * early + prefill_rank, -1),
        tensor_count * early,
    )
    payload, own_score = attention_partials(
        decode_queries, new_keys, cache_keys, cache_values, group_of, cache_lengths,
        out_weight.shape[0],
    )
    payload, first_in = lax.optimization_barrier((payload, first_in))
    first_done = experts_on(first_in, experts)
    decode_hidden = attention_finish(payload, own_score, new_values, decode_residual, out_weight)
    decode_float, decode_normed = rms_normed(decode_hidden, norm_gain)
    late_slot = jnp.concatenate(
        [
            jnp.where(
                prefill_rank >= early, prefill_routes * late + prefill_rank - early, -1
            ),
            decode_routes * late + overflow[decode_routes] + decode_rank,
        ]
    )
    second_in = dispatch(
        jnp.concatenate([prefill_normed, decode_normed], axis=0), late_slot, tensor_count * late
    )
    first_done, second_in = lax.optimization_barrier((first_done, second_in))
    first_back = give_back(first_done)
    second_done = experts_on(second_in, experts)
    first_back, second_done = lax.optimization_barrier((first_back, second_done))
    second_back = give_back(second_done)
    returned = jnp.concatenate([first_back, second_back], axis=1).reshape(
        tensor_count * stride, model_width
    )
    place = jnp.concatenate(
        [
            prefill_routes * stride + prefill_rank,
            decode_routes * stride + early + overflow[decode_routes] + decode_rank,
        ]
    ).reshape(row_count, top_count)
    columns = jnp.arange(tensor_count * stride, dtype=jnp.int32)
    mixing = jnp.sum(
        jnp.where(place[:, :, None] == columns[None, None, :], route_weights[:, :, None], 0.0),
        axis=1,
    )
    high = mixing.astype(jnp.bfloat16)
    rest = mixing - high.astype(jnp.float32)
    middle = rest.astype(jnp.bfloat16)
    low = (rest - middle.astype(jnp.float32)).astype(jnp.bfloat16)

    def combined(lo, hi, row_float):
        parts = jnp.dot(
            jnp.concatenate([high[lo:hi], middle[lo:hi], low[lo:hi]], axis=0),
            returned,
            preferred_element_type=jnp.float32,
        ).reshape(3, hi - lo, model_width)
        weighted = (parts[0] + parts[1]) + parts[2]
        return (row_float + weighted).astype(jnp.bfloat16)

    return (
        combined(0, prefill_count, prefill_float),
        combined(prefill_count, row_count, decode_float)[None],
    )


def solution(mesh):
    in_specs = (
        P("dp", None, None),
        P("dp", None, None),
        P("dp", None, None),
        P("dp", None, "tensor", None),
        P("dp", None, "tensor", None),
        P("dp", None),
        P("dp", None),
        P("dp", "tensor", None),
        P("tensor", None),
        P(("dp", "tensor"), None),
        P(),
        P(("dp", "tensor"), None),
        P(("dp", "tensor"), None),
        P("tensor", None, "dp"),
        P("tensor", None, "dp"),
        P("tensor", "dp", None),
    )
    out_specs = (P(("dp", "tensor"), None), P("dp", "tensor", None))
    return jax.shard_map(
        per_device, mesh=mesh, in_specs=in_specs, out_specs=out_specs, check_vma=False
    )
```

```python
import math

import jax
import jax.numpy as jnp
from jax import lax
from jax.sharding import PartitionSpec as P

HEADS = 16
HEAD_DIM = 128


def expert_mlp(inputs, gate_w, up_w, down_w):
    flat_rows = inputs.reshape(-1, inputs.shape[-1])
    gate = jnp.dot(flat_rows, gate_w, preferred_element_type=jnp.float32)
    upper = jnp.dot(flat_rows, up_w, preferred_element_type=jnp.float32)
    active = (jax.nn.silu(gate) * upper).astype(jnp.bfloat16)
    return jnp.dot(active, down_w, preferred_element_type=jnp.float32)


def attention_partials(
    decode_queries, new_keys, cache_keys, cache_values, group_of, cache_lengths, width
):
    tensor_count = lax.axis_size("tensor")
    tensor_rank = lax.axis_index("tensor")
    requests = decode_queries.shape[1]
    groups = cache_keys.shape[1]
    reach = cache_keys.shape[2]
    model_width = decode_queries.shape[2]
    assert HEAD_DIM % width == 0
    factor = 1.0 / math.sqrt(HEAD_DIM)
    query_heads = decode_queries[0].reshape(requests, HEADS, HEAD_DIM)
    key_table = cache_keys[0].reshape(groups, reach, HEADS, HEAD_DIM)
    value_table = cache_values[0].reshape(groups, reach, HEADS, HEAD_DIM)
    scores = (
        jnp.einsum("rhd,gjhd->grhj", query_heads, key_table, preferred_element_type=jnp.float32)
        * factor
    )
    positions = tensor_rank * reach + jnp.arange(reach, dtype=jnp.int32)
    member = group_of[0][None, :] == jnp.arange(groups, dtype=jnp.int32)[:, None]
    within = positions[None, :] < cache_lengths[0][:, None]
    visible = (member[:, :, None] & within[:, None, :])[:, :, None, :]
    own_keys = new_keys[0].astype(jnp.float32).reshape(requests, HEADS, HEAD_DIM)
    own_score = jnp.sum(query_heads.astype(jnp.float32) * own_keys, axis=2) * factor
    local_peak = jnp.maximum(jnp.max(jnp.where(visible, scores, -jnp.inf), axis=(0, 3)), own_score)
    expon = jnp.where(visible, jnp.exp(scores - local_peak[None, :, :, None]), 0.0)
    probs = expon.astype(jnp.bfloat16)
    local_totals = jnp.sum(expon, axis=(0, 3))
    mixture = jnp.einsum(
        "grhj,gjhd->rhd", probs, value_table, preferred_element_type=jnp.float32
    ).reshape(requests, tensor_count, width)
    head_of = (jnp.arange(tensor_count, dtype=jnp.int32) * width) // HEAD_DIM
    peak_to = local_peak.T[head_of]
    totals_to = local_totals.T[head_of]
    flat_mix = jnp.transpose(mixture, (1, 0, 2)).reshape(tensor_count, requests * width)
    payload = jnp.concatenate([flat_mix, peak_to, totals_to], axis=1)
    return payload, own_score


def attention_finish(payload, own_score, new_values, decode_residual, out_weight):
    tensor_count = lax.axis_size("tensor")
    tensor_rank = lax.axis_index("tensor")
    requests, model_width = new_values.shape[1], new_values.shape[2]
    width = out_weight.shape[0]
    received = lax.all_to_all(payload, "tensor", 0, 0, tiled=True)
    mixed_width = requests * width
    part_mix = received[:, :mixed_width].reshape(tensor_count, requests, width)
    part_peak = received[:, mixed_width:mixed_width + requests]
    part_totals = received[:, mixed_width + requests:]
    peak = jnp.max(part_peak, axis=0)
    scale = jnp.exp(part_peak - peak[None, :])
    my_head = (tensor_rank * width) // HEAD_DIM
    first_column = tensor_rank * width
    own_here = lax.dynamic_index_in_dim(own_score, my_head, axis=1, keepdims=False)
    own_exp = jnp.exp(own_here - peak)
    own_prob = lax.optimization_barrier(own_exp.astype(jnp.bfloat16)).astype(jnp.float32)
    totals = jnp.sum(scale * part_totals, axis=0) + own_exp
    own_values = lax.dynamic_slice_in_dim(new_values[0], first_column, width, 1).astype(jnp.float32)
    summed_mix = jnp.sum(scale[:, :, None] * part_mix, axis=0) + own_prob[:, None] * own_values
    attended = (summed_mix / totals[:, None]).astype(jnp.bfloat16)
    partial = jnp.dot(attended, out_weight, preferred_element_type=jnp.float32)
    per_device = requests // tensor_count
    gathered = lax.all_to_all(
        partial.astype(jnp.bfloat16).reshape(tensor_count, per_device, model_width),
        "tensor", 0, 0, tiled=True,
    )
    projected = jnp.sum(gathered.astype(jnp.float32), axis=0)
    return (decode_residual[0].astype(jnp.float32) + projected).astype(jnp.bfloat16)


def rms_normed(residual_rows, norm_gain):
    row_float = residual_rows.astype(jnp.float32)
    inverse = lax.rsqrt(jnp.mean(row_float * row_float, axis=1, keepdims=True) + 1e-06)
    return row_float, (row_float * inverse * norm_gain).astype(jnp.bfloat16)


def dispatch(normed, slot_index, slot_count):
    row_count = normed.shape[0]
    slots = jnp.arange(slot_count, dtype=jnp.int32)
    select = jnp.any(
        slot_index.reshape(row_count, -1)[None, :, :] == slots[:, None, None], axis=2
    ).astype(jnp.bfloat16)
    outgoing = jnp.dot(select, normed, preferred_element_type=jnp.float32).astype(jnp.bfloat16)
    tensor_count = lax.axis_size("tensor")
    outgoing = outgoing.reshape(tensor_count, slot_count // tensor_count, normed.shape[1])
    return lax.all_to_all(outgoing, "tensor", split_axis=0, concat_axis=0, tiled=True)


def experts_on(received, experts, norm_gain):
    block = lax.all_gather(received, "dp", axis=0, tiled=True)
    _, normed = rms_normed(block.reshape(-1, block.shape[-1]), norm_gain)
    return expert_mlp(normed, *experts).reshape(block.shape).astype(jnp.bfloat16)


def rank_in_expert(flat_expert, tensor_count):
    one_hot = (flat_expert[:, None] == jnp.arange(tensor_count, dtype=jnp.int32)[None, :]).astype(
        jnp.int32
    )
    count = flat_expert.shape[0]
    lower = (
        jnp.arange(count, dtype=jnp.int32)[:, None] > jnp.arange(count, dtype=jnp.int32)[None, :]
    ).astype(jnp.bfloat16)
    earlier = jnp.dot(
        lower, one_hot.astype(jnp.bfloat16), preferred_element_type=jnp.float32
    ).astype(jnp.int32)
    return jnp.sum(earlier * one_hot, axis=1), jnp.sum(one_hot, axis=0)


def give_back(done):
    return lax.all_to_all(
        lax.psum_scatter(done, "dp", scatter_dimension=0, tiled=True),
        "tensor",
        split_axis=0,
        concat_axis=0,
        tiled=True,
    )


def per_device(
    decode_queries,
    new_keys,
    new_values,
    cache_keys,
    cache_values,
    group_of,
    cache_lengths,
    decode_residual,
    out_weight,
    prefill_states,
    norm_gain,
    routes,
    route_weights,
    w_gate,
    w_up,
    w_down,
):
    tensor_count = lax.axis_size("tensor")
    model_width = decode_queries.shape[2]
    prefill_count = prefill_states.shape[0]
    row_count, top_count = routes.shape
    decode_count = row_count - prefill_count
    capacity = max(8, (row_count * top_count * 3 // (2 * tensor_count) + 7) // 8 * 8)
    early = max(8, capacity * 2 // 3 // 8 * 8)
    late = max(capacity - early, decode_count)
    stride = early + late
    experts = (w_gate[0], w_up[0], w_down[0])
    prefill_routes = routes[:prefill_count].reshape(-1)
    decode_routes = routes[prefill_count:].reshape(-1)
    prefill_rank, prefill_counts = rank_in_expert(prefill_routes, tensor_count)
    decode_rank, _ = rank_in_expert(decode_routes, tensor_count)
    overflow = jnp.maximum(prefill_counts - early, 0)
    prefill_float = prefill_states.astype(jnp.float32)
    first_in = dispatch(
        prefill_states,
        jnp.where(prefill_rank < early, prefill_routes * early + prefill_rank, -1),
        tensor_count * early,
    )
    payload, own_score = attention_partials(
        decode_queries, new_keys, cache_keys, cache_values, group_of, cache_lengths,
        out_weight.shape[0],
    )
    payload, first_in = lax.optimization_barrier((payload, first_in))
    first_done = experts_on(first_in, experts, norm_gain)
    decode_hidden = attention_finish(payload, own_score, new_values, decode_residual, out_weight)
    decode_float = decode_hidden.astype(jnp.float32)
    late_slot = jnp.concatenate(
        [
            jnp.where(
                prefill_rank >= early, prefill_routes * late + prefill_rank - early, -1
            ),
            decode_routes * late + overflow[decode_routes] + decode_rank,
        ]
    )
    second_in = dispatch(
        jnp.concatenate([prefill_states, decode_hidden], axis=0), late_slot, tensor_count * late
    )
    first_done, second_in = lax.optimization_barrier((first_done, second_in))
    first_back = give_back(first_done)
    second_done = experts_on(second_in, experts, norm_gain)
    first_back, second_done = lax.optimization_barrier((first_back, second_done))
    second_back = give_back(second_done)
    returned = jnp.concatenate([first_back, second_back], axis=1).reshape(
        tensor_count * stride, model_width
    )
    place = jnp.concatenate(
        [
            prefill_routes * stride + prefill_rank,
            decode_routes * stride + early + overflow[decode_routes] + decode_rank,
        ]
    ).reshape(row_count, top_count)
    columns = jnp.arange(tensor_count * stride, dtype=jnp.int32)
    mixing = jnp.sum(
        jnp.where(place[:, :, None] == columns[None, None, :], route_weights[:, :, None], 0.0),
        axis=1,
    )
    high = mixing.astype(jnp.bfloat16)
    rest = mixing - high.astype(jnp.float32)
    middle = rest.astype(jnp.bfloat16)
    low = (rest - middle.astype(jnp.float32)).astype(jnp.bfloat16)

    def combined(lo, hi, row_float):
        parts = jnp.dot(
            jnp.concatenate([high[lo:hi], middle[lo:hi], low[lo:hi]], axis=0),
            returned,
            preferred_element_type=jnp.float32,
        ).reshape(3, hi - lo, model_width)
        weighted = (parts[0] + parts[1]) + parts[2]
        return (row_float + weighted).astype(jnp.bfloat16)

    return (
        combined(0, prefill_count, prefill_float),
        combined(prefill_count, row_count, decode_float)[None],
    )


def solution(mesh):
    in_specs = (
        P("dp", None, None),
        P("dp", None, None),
        P("dp", None, None),
        P("dp", None, "tensor", None),
        P("dp", None, "tensor", None),
        P("dp", None),
        P("dp", None),
        P("dp", "tensor", None),
        P("tensor", None),
        P(("dp", "tensor"), None),
        P(),
        P(("dp", "tensor"), None),
        P(("dp", "tensor"), None),
        P("tensor", None, "dp"),
        P("tensor", None, "dp"),
        P("tensor", "dp", None),
    )
    out_specs = (P(("dp", "tensor"), None), P("dp", "tensor", None))
    return jax.shard_map(
        per_device, mesh=mesh, in_specs=in_specs, out_specs=out_specs, check_vma=False
    )
```

```python
import math

import jax
import jax.numpy as jnp
from jax import lax
from jax.sharding import PartitionSpec as P

HEADS = 16
HEAD_DIM = 128


def expert_mlp(inputs, gate_w, up_w, down_w):
    flat_rows = inputs.reshape(-1, inputs.shape[-1])
    gate = jnp.dot(flat_rows, gate_w, preferred_element_type=jnp.float32)
    upper = jnp.dot(flat_rows, up_w, preferred_element_type=jnp.float32)
    active = (jax.nn.silu(gate) * upper).astype(jnp.bfloat16)
    return jnp.dot(active, down_w, preferred_element_type=jnp.float32)


def attention_partials(
    decode_queries, new_keys, cache_keys, cache_values, group_of, cache_lengths, width
):
    tensor_count = lax.axis_size("tensor")
    tensor_rank = lax.axis_index("tensor")
    requests = decode_queries.shape[1]
    groups = cache_keys.shape[1]
    reach = cache_keys.shape[2]
    model_width = decode_queries.shape[2]
    assert HEAD_DIM % width == 0
    factor = 1.0 / math.sqrt(HEAD_DIM)
    query_heads = decode_queries[0].reshape(requests, HEADS, HEAD_DIM)
    key_table = cache_keys[0].reshape(groups, reach, HEADS, HEAD_DIM)
    value_table = cache_values[0].reshape(groups, reach, HEADS, HEAD_DIM)
    scores = (
        jnp.einsum("rhd,gjhd->grhj", query_heads, key_table, preferred_element_type=jnp.float32)
        * factor
    )
    positions = tensor_rank * reach + jnp.arange(reach, dtype=jnp.int32)
    member = group_of[0][None, :] == jnp.arange(groups, dtype=jnp.int32)[:, None]
    within = positions[None, :] < cache_lengths[0][:, None]
    visible = (member[:, :, None] & within[:, None, :])[:, :, None, :]
    own_keys = new_keys[0].astype(jnp.float32).reshape(requests, HEADS, HEAD_DIM)
    own_score = jnp.sum(query_heads.astype(jnp.float32) * own_keys, axis=2) * factor
    local_peak = jnp.maximum(jnp.max(jnp.where(visible, scores, -jnp.inf), axis=(0, 3)), own_score)
    expon = jnp.where(visible, jnp.exp(scores - local_peak[None, :, :, None]), 0.0)
    probs = expon.astype(jnp.bfloat16)
    local_totals = jnp.sum(expon, axis=(0, 3))
    mixture = jnp.einsum(
        "grhj,gjhd->rhd", probs, value_table, preferred_element_type=jnp.float32
    ).reshape(requests, tensor_count, width)
    head_of = (jnp.arange(tensor_count, dtype=jnp.int32) * width) // HEAD_DIM
    peak_to = local_peak.T[head_of]
    totals_to = local_totals.T[head_of]
    flat_mix = jnp.transpose(mixture, (1, 0, 2)).reshape(tensor_count, requests * width)
    payload = jnp.concatenate([flat_mix, peak_to, totals_to], axis=1)
    return payload, own_score


def attention_finish(payload, own_score, new_values, decode_residual, out_weight):
    tensor_count = lax.axis_size("tensor")
    tensor_rank = lax.axis_index("tensor")
    requests, model_width = new_values.shape[1], new_values.shape[2]
    width = out_weight.shape[0]
    received = lax.all_to_all(payload, "tensor", 0, 0, tiled=True)
    mixed_width = requests * width
    part_mix = received[:, :mixed_width].reshape(tensor_count, requests, width)
    part_peak = received[:, mixed_width:mixed_width + requests]
    part_totals = received[:, mixed_width + requests:]
    peak = jnp.max(part_peak, axis=0)
    scale = jnp.exp(part_peak - peak[None, :])
    my_head = (tensor_rank * width) // HEAD_DIM
    first_column = tensor_rank * width
    own_here = lax.dynamic_index_in_dim(own_score, my_head, axis=1, keepdims=False)
    own_exp = jnp.exp(own_here - peak)
    own_prob = lax.optimization_barrier(own_exp.astype(jnp.bfloat16)).astype(jnp.float32)
    totals = jnp.sum(scale * part_totals, axis=0) + own_exp
    own_values = lax.dynamic_slice_in_dim(new_values[0], first_column, width, 1).astype(jnp.float32)
    summed_mix = jnp.sum(scale[:, :, None] * part_mix, axis=0) + own_prob[:, None] * own_values
    attended = (summed_mix / totals[:, None]).astype(jnp.bfloat16)
    partial = jnp.dot(attended, out_weight, preferred_element_type=jnp.float32)
    per_device = requests // tensor_count
    gathered = lax.all_to_all(
        partial.astype(jnp.bfloat16).reshape(tensor_count, per_device, model_width),
        "tensor", 0, 0, tiled=True,
    )
    projected = jnp.sum(gathered.astype(jnp.float32), axis=0)
    return (decode_residual[0].astype(jnp.float32) + projected).astype(jnp.bfloat16)


def rms_normed(residual_rows, norm_gain):
    row_float = residual_rows.astype(jnp.float32)
    inverse = lax.rsqrt(jnp.mean(row_float * row_float, axis=1, keepdims=True) + 1e-06)
    return row_float, (row_float * inverse * norm_gain).astype(jnp.bfloat16)


def dispatch(normed, slot_index, slot_count):
    row_count = normed.shape[0]
    slots = jnp.arange(slot_count, dtype=jnp.int32)
    select = jnp.any(
        slot_index.reshape(row_count, -1)[None, :, :] == slots[:, None, None], axis=2
    ).astype(jnp.bfloat16)
    outgoing = jnp.dot(select, normed, preferred_element_type=jnp.float32).astype(jnp.bfloat16)
    tensor_count = lax.axis_size("tensor")
    outgoing = outgoing.reshape(tensor_count, slot_count // tensor_count, normed.shape[1])
    return lax.all_to_all(outgoing, "tensor", split_axis=0, concat_axis=0, tiled=True)


def dispatch_two(early_rows, early_slots, late_rows, late_slots, slot_count):
    def picked(rows, slot_index):
        slots = jnp.arange(slot_count, dtype=jnp.int32)
        select = jnp.any(
            slot_index.reshape(rows.shape[0], -1)[None, :, :] == slots[:, None, None], axis=2
        ).astype(jnp.bfloat16)
        return jnp.dot(select, rows, preferred_element_type=jnp.float32)

    outgoing = (picked(early_rows, early_slots) + picked(late_rows, late_slots)).astype(jnp.bfloat16)
    tensor_count = lax.axis_size("tensor")
    outgoing = outgoing.reshape(tensor_count, slot_count // tensor_count, early_rows.shape[1])
    return lax.all_to_all(outgoing, "tensor", split_axis=0, concat_axis=0, tiled=True)


def experts_on(received, experts, norm_gain):
    block = lax.all_gather(received, "dp", axis=0, tiled=True)
    _, normed = rms_normed(block.reshape(-1, block.shape[-1]), norm_gain)
    return expert_mlp(normed, *experts).reshape(block.shape).astype(jnp.bfloat16)


def rank_in_expert(flat_expert, tensor_count):
    one_hot = (flat_expert[:, None] == jnp.arange(tensor_count, dtype=jnp.int32)[None, :]).astype(
        jnp.int32
    )
    count = flat_expert.shape[0]
    lower = (
        jnp.arange(count, dtype=jnp.int32)[:, None] > jnp.arange(count, dtype=jnp.int32)[None, :]
    ).astype(jnp.bfloat16)
    earlier = jnp.dot(
        lower, one_hot.astype(jnp.bfloat16), preferred_element_type=jnp.float32
    ).astype(jnp.int32)
    return jnp.sum(earlier * one_hot, axis=1), jnp.sum(one_hot, axis=0)


def give_back(done):
    return lax.all_to_all(
        lax.psum_scatter(done, "dp", scatter_dimension=0, tiled=True),
        "tensor",
        split_axis=0,
        concat_axis=0,
        tiled=True,
    )


def per_device(
    decode_queries,
    new_keys,
    new_values,
    cache_keys,
    cache_values,
    group_of,
    cache_lengths,
    decode_residual,
    out_weight,
    prefill_states,
    norm_gain,
    routes,
    route_weights,
    w_gate,
    w_up,
    w_down,
):
    tensor_count = lax.axis_size("tensor")
    model_width = decode_queries.shape[2]
    prefill_count = prefill_states.shape[0]
    row_count, top_count = routes.shape
    decode_count = row_count - prefill_count
    capacity = max(8, (row_count * top_count * 3 // (2 * tensor_count) + 7) // 8 * 8)
    early = max(8, capacity * 2 // 3 // 8 * 8)
    late = max(capacity - early, decode_count)
    stride = early + late
    experts = (w_gate[0], w_up[0], w_down[0])
    prefill_routes = routes[:prefill_count].reshape(-1)
    decode_routes = routes[prefill_count:].reshape(-1)
    prefill_rank, prefill_counts = rank_in_expert(prefill_routes, tensor_count)
    decode_rank, _ = rank_in_expert(decode_routes, tensor_count)
    overflow = jnp.maximum(prefill_counts - early, 0)
    prefill_float = prefill_states.astype(jnp.float32)
    first_in = dispatch(
        prefill_states,
        jnp.where(prefill_rank < early, prefill_routes * early + prefill_rank, -1),
        tensor_count * early,
    )
    payload, own_score = attention_partials(
        decode_queries, new_keys, cache_keys, cache_values, group_of, cache_lengths,
        out_weight.shape[0],
    )
    payload, first_in = lax.optimization_barrier((payload, first_in))
    first_done = experts_on(first_in, experts, norm_gain)
    decode_hidden = attention_finish(payload, own_score, new_values, decode_residual, out_weight)
    decode_float = decode_hidden.astype(jnp.float32)
    late_slot = jnp.concatenate(
        [
            jnp.where(
                prefill_rank >= early, prefill_routes * late + prefill_rank - early, -1
            ),
            decode_routes * late + overflow[decode_routes] + decode_rank,
        ]
    )
    second_in = dispatch_two(
        prefill_states, late_slot[:prefill_count * top_count],
        decode_hidden, late_slot[prefill_count * top_count:], tensor_count * late,
    )
    first_done, second_in = lax.optimization_barrier((first_done, second_in))
    first_back = give_back(first_done)
    second_done = experts_on(second_in, experts, norm_gain)
    first_back, second_done = lax.optimization_barrier((first_back, second_done))
    second_back = give_back(second_done)
    returned = jnp.concatenate([first_back, second_back], axis=1).reshape(
        tensor_count * stride, model_width
    )
    place = jnp.concatenate(
        [
            prefill_routes * stride + prefill_rank,
            decode_routes * stride + early + overflow[decode_routes] + decode_rank,
        ]
    ).reshape(row_count, top_count)
    columns = jnp.arange(tensor_count * stride, dtype=jnp.int32)
    mixing = jnp.sum(
        jnp.where(place[:, :, None] == columns[None, None, :], route_weights[:, :, None], 0.0),
        axis=1,
    )
    high = mixing.astype(jnp.bfloat16)
    rest = mixing - high.astype(jnp.float32)
    middle = rest.astype(jnp.bfloat16)
    low = (rest - middle.astype(jnp.float32)).astype(jnp.bfloat16)

    def combined(lo, hi, row_float):
        parts = jnp.dot(
            jnp.concatenate([high[lo:hi], middle[lo:hi], low[lo:hi]], axis=0),
            returned,
            preferred_element_type=jnp.float32,
        ).reshape(3, hi - lo, model_width)
        weighted = (parts[0] + parts[1]) + parts[2]
        return (row_float + weighted).astype(jnp.bfloat16)

    return (
        combined(0, prefill_count, prefill_float),
        combined(prefill_count, row_count, decode_float)[None],
    )


def solution(mesh):
    in_specs = (
        P("dp", None, None),
        P("dp", None, None),
        P("dp", None, None),
        P("dp", None, "tensor", None),
        P("dp", None, "tensor", None),
        P("dp", None),
        P("dp", None),
        P("dp", "tensor", None),
        P("tensor", None),
        P(("dp", "tensor"), None),
        P(),
        P(("dp", "tensor"), None),
        P(("dp", "tensor"), None),
        P("tensor", None, "dp"),
        P("tensor", None, "dp"),
        P("tensor", "dp", None),
    )
    out_specs = (P(("dp", "tensor"), None), P("dp", "tensor", None))
    return jax.shard_map(
        per_device, mesh=mesh, in_specs=in_specs, out_specs=out_specs, check_vma=False
    )
```

```python
import math

import jax
import jax.numpy as jnp
from jax import lax
from jax.sharding import PartitionSpec as P

HEADS = 16
HEAD_DIM = 128


def expert_mlp(inputs, gate_w, up_w, down_w):
    flat_rows = inputs.reshape(-1, inputs.shape[-1])
    gate = jnp.dot(flat_rows, gate_w, preferred_element_type=jnp.float32)
    upper = jnp.dot(flat_rows, up_w, preferred_element_type=jnp.float32)
    active = (jax.nn.silu(gate) * upper).astype(jnp.bfloat16)
    return jnp.dot(active, down_w, preferred_element_type=jnp.float32)


def attention_partials(
    decode_queries, new_keys, cache_keys, cache_values, group_of, cache_lengths, width
):
    tensor_count = lax.axis_size("tensor")
    tensor_rank = lax.axis_index("tensor")
    requests = decode_queries.shape[1]
    groups = cache_keys.shape[1]
    reach = cache_keys.shape[2]
    model_width = decode_queries.shape[2]
    assert HEAD_DIM % width == 0
    factor = 1.0 / math.sqrt(HEAD_DIM)
    query_heads = decode_queries[0].reshape(requests, HEADS, HEAD_DIM)
    key_table = cache_keys[0].reshape(groups, reach, HEADS, HEAD_DIM)
    value_table = cache_values[0].reshape(groups, reach, HEADS, HEAD_DIM)
    scores = (
        jnp.einsum("rhd,gjhd->grhj", query_heads, key_table, preferred_element_type=jnp.float32)
        * factor
    )
    positions = tensor_rank * reach + jnp.arange(reach, dtype=jnp.int32)
    member = group_of[0][None, :] == jnp.arange(groups, dtype=jnp.int32)[:, None]
    within = positions[None, :] < cache_lengths[0][:, None]
    visible = (member[:, :, None] & within[:, None, :])[:, :, None, :]
    own_keys = new_keys[0].astype(jnp.float32).reshape(requests, HEADS, HEAD_DIM)
    own_score = jnp.sum(query_heads.astype(jnp.float32) * own_keys, axis=2) * factor
    local_peak = jnp.maximum(jnp.max(jnp.where(visible, scores, -jnp.inf), axis=(0, 3)), own_score)
    expon = jnp.where(visible, jnp.exp(scores - local_peak[None, :, :, None]), 0.0)
    probs = expon.astype(jnp.bfloat16)
    local_totals = jnp.sum(expon, axis=(0, 3))
    mixture = jnp.einsum(
        "grhj,gjhd->rhd", probs, value_table, preferred_element_type=jnp.float32
    ).reshape(requests, tensor_count, width)
    head_of = (jnp.arange(tensor_count, dtype=jnp.int32) * width) // HEAD_DIM
    peak_to = local_peak.T[head_of]
    totals_to = local_totals.T[head_of]
    flat_mix = jnp.transpose(mixture, (1, 0, 2)).reshape(tensor_count, requests * width)
    payload = jnp.concatenate([flat_mix, peak_to, totals_to], axis=1)
    return payload, own_score


def attention_finish(payload, own_score, new_values, decode_residual, out_weight):
    tensor_count = lax.axis_size("tensor")
    tensor_rank = lax.axis_index("tensor")
    requests, model_width = new_values.shape[1], new_values.shape[2]
    width = out_weight.shape[0]
    received = lax.all_to_all(payload, "tensor", 0, 0, tiled=True)
    mixed_width = requests * width
    part_mix = received[:, :mixed_width].reshape(tensor_count, requests, width)
    part_peak = received[:, mixed_width:mixed_width + requests]
    part_totals = received[:, mixed_width + requests:]
    peak = jnp.max(part_peak, axis=0)
    scale = jnp.exp(part_peak - peak[None, :])
    my_head = (tensor_rank * width) // HEAD_DIM
    first_column = tensor_rank * width
    own_here = lax.dynamic_index_in_dim(own_score, my_head, axis=1, keepdims=False)
    own_exp = jnp.exp(own_here - peak)
    own_prob = lax.optimization_barrier(own_exp.astype(jnp.bfloat16)).astype(jnp.float32)
    totals = jnp.sum(scale * part_totals, axis=0) + own_exp
    own_values = lax.dynamic_slice_in_dim(new_values[0], first_column, width, 1).astype(jnp.float32)
    summed_mix = jnp.sum(scale[:, :, None] * part_mix, axis=0) + own_prob[:, None] * own_values
    attended = (summed_mix / totals[:, None]).astype(jnp.bfloat16)
    partial = jnp.dot(attended, out_weight, preferred_element_type=jnp.float32)
    per_device = requests // tensor_count
    gathered = lax.all_to_all(
        partial.astype(jnp.bfloat16).reshape(tensor_count, per_device, model_width),
        "tensor", 0, 0, tiled=True,
    )
    projected = jnp.sum(gathered.astype(jnp.float32), axis=0)
    return (decode_residual[0].astype(jnp.float32) + projected).astype(jnp.bfloat16)


def rms_normed(residual_rows, norm_gain):
    row_float = residual_rows.astype(jnp.float32)
    inverse = lax.rsqrt(jnp.mean(row_float * row_float, axis=1, keepdims=True) + 1e-06)
    return row_float, (row_float * inverse * norm_gain).astype(jnp.bfloat16)


def dispatch(normed, slot_index, slot_count):
    row_count = normed.shape[0]
    slots = jnp.arange(slot_count, dtype=jnp.int32)
    select = jnp.any(
        slot_index.reshape(row_count, -1)[None, :, :] == slots[:, None, None], axis=2
    ).astype(jnp.bfloat16)
    outgoing = jnp.dot(select, normed, preferred_element_type=jnp.float32).astype(jnp.bfloat16)
    tensor_count = lax.axis_size("tensor")
    outgoing = outgoing.reshape(tensor_count, slot_count // tensor_count, normed.shape[1])
    return lax.all_to_all(outgoing, "tensor", split_axis=0, concat_axis=0, tiled=True)


def experts_on(received, experts, norm_gain):
    block = lax.all_gather(received, "dp", axis=0, tiled=True)
    _, normed = rms_normed(block.reshape(-1, block.shape[-1]), norm_gain)
    return expert_mlp(normed, *experts).reshape(block.shape).astype(jnp.bfloat16)


def rank_in_expert(flat_expert, tensor_count):
    one_hot = (flat_expert[:, None] == jnp.arange(tensor_count, dtype=jnp.int32)[None, :]).astype(
        jnp.int32
    )
    count = flat_expert.shape[0]
    lower = (
        jnp.arange(count, dtype=jnp.int32)[:, None] > jnp.arange(count, dtype=jnp.int32)[None, :]
    ).astype(jnp.bfloat16)
    earlier = jnp.dot(
        lower, one_hot.astype(jnp.bfloat16), preferred_element_type=jnp.float32
    ).astype(jnp.int32)
    return jnp.sum(earlier * one_hot, axis=1), jnp.sum(one_hot, axis=0)


def give_back(done):
    return lax.all_to_all(
        lax.psum_scatter(done, "dp", scatter_dimension=0, tiled=True),
        "tensor",
        split_axis=0,
        concat_axis=0,
        tiled=True,
    )


def per_device(
    decode_queries,
    new_keys,
    new_values,
    cache_keys,
    cache_values,
    group_of,
    cache_lengths,
    decode_residual,
    out_weight,
    prefill_states,
    norm_gain,
    routes,
    route_weights,
    w_gate,
    w_up,
    w_down,
):
    tensor_count = lax.axis_size("tensor")
    model_width = decode_queries.shape[2]
    prefill_count = prefill_states.shape[0]
    row_count, top_count = routes.shape
    decode_count = row_count - prefill_count
    capacity = max(8, (row_count * top_count * 3 // (2 * tensor_count) + 7) // 8 * 8)
    early = max(8, capacity // 3 // 8 * 8)
    late = max(capacity - early, decode_count)
    stride = early + late
    experts = (w_gate[0], w_up[0], w_down[0])
    prefill_routes = routes[:prefill_count].reshape(-1)
    decode_routes = routes[prefill_count:].reshape(-1)
    prefill_rank, prefill_counts = rank_in_expert(prefill_routes, tensor_count)
    decode_rank, _ = rank_in_expert(decode_routes, tensor_count)
    overflow = jnp.maximum(prefill_counts - early, 0)
    prefill_float = prefill_states.astype(jnp.float32)
    first_in = dispatch(
        prefill_states,
        jnp.where(prefill_rank < early, prefill_routes * early + prefill_rank, -1),
        tensor_count * early,
    )
    payload, own_score = attention_partials(
        decode_queries, new_keys, cache_keys, cache_values, group_of, cache_lengths,
        out_weight.shape[0],
    )
    payload, first_in = lax.optimization_barrier((payload, first_in))
    first_done = experts_on(first_in, experts, norm_gain)
    decode_hidden = attention_finish(payload, own_score, new_values, decode_residual, out_weight)
    decode_float = decode_hidden.astype(jnp.float32)
    late_slot = jnp.concatenate(
        [
            jnp.where(
                prefill_rank >= early, prefill_routes * late + prefill_rank - early, -1
            ),
            decode_routes * late + overflow[decode_routes] + decode_rank,
        ]
    )
    second_in = dispatch(
        jnp.concatenate([prefill_states, decode_hidden], axis=0), late_slot, tensor_count * late
    )
    first_done, second_in = lax.optimization_barrier((first_done, second_in))
    first_back = give_back(first_done)
    second_done = experts_on(second_in, experts, norm_gain)
    first_back, second_done = lax.optimization_barrier((first_back, second_done))
    second_back = give_back(second_done)
    returned = jnp.concatenate([first_back, second_back], axis=1).reshape(
        tensor_count * stride, model_width
    )
    place = jnp.concatenate(
        [
            prefill_routes * stride + prefill_rank,
            decode_routes * stride + early + overflow[decode_routes] + decode_rank,
        ]
    ).reshape(row_count, top_count)
    columns = jnp.arange(tensor_count * stride, dtype=jnp.int32)
    mixing = jnp.sum(
        jnp.where(place[:, :, None] == columns[None, None, :], route_weights[:, :, None], 0.0),
        axis=1,
    )
    high = mixing.astype(jnp.bfloat16)
    rest = mixing - high.astype(jnp.float32)
    middle = rest.astype(jnp.bfloat16)
    low = (rest - middle.astype(jnp.float32)).astype(jnp.bfloat16)

    def combined(lo, hi, row_float):
        parts = jnp.dot(
            jnp.concatenate([high[lo:hi], middle[lo:hi], low[lo:hi]], axis=0),
            returned,
            preferred_element_type=jnp.float32,
        ).reshape(3, hi - lo, model_width)
        weighted = (parts[0] + parts[1]) + parts[2]
        return (row_float + weighted).astype(jnp.bfloat16)

    return (
        combined(0, prefill_count, prefill_float),
        combined(prefill_count, row_count, decode_float)[None],
    )


def solution(mesh):
    in_specs = (
        P("dp", None, None),
        P("dp", None, None),
        P("dp", None, None),
        P("dp", None, "tensor", None),
        P("dp", None, "tensor", None),
        P("dp", None),
        P("dp", None),
        P("dp", "tensor", None),
        P("tensor", None),
        P(("dp", "tensor"), None),
        P(),
        P(("dp", "tensor"), None),
        P(("dp", "tensor"), None),
        P("tensor", None, "dp"),
        P("tensor", None, "dp"),
        P("tensor", "dp", None),
    )
    out_specs = (P(("dp", "tensor"), None), P("dp", "tensor", None))
    return jax.shard_map(
        per_device, mesh=mesh, in_specs=in_specs, out_specs=out_specs, check_vma=False
    )
```

```python
import math

import jax
import jax.numpy as jnp
from jax import lax
from jax.sharding import PartitionSpec as P

HEADS = 16
HEAD_DIM = 128


def expert_mlp(inputs, gate_w, up_w, down_w):
    flat_rows = inputs.reshape(-1, inputs.shape[-1])
    gate = jnp.dot(flat_rows, gate_w, preferred_element_type=jnp.float32)
    upper = jnp.dot(flat_rows, up_w, preferred_element_type=jnp.float32)
    active = (jax.nn.silu(gate) * upper).astype(jnp.bfloat16)
    return jnp.dot(active, down_w, preferred_element_type=jnp.float32)


def attention_partials(
    decode_queries, new_keys, cache_keys, cache_values, group_of, cache_lengths, width
):
    tensor_count = lax.axis_size("tensor")
    tensor_rank = lax.axis_index("tensor")
    requests = decode_queries.shape[1]
    groups = cache_keys.shape[1]
    reach = cache_keys.shape[2]
    model_width = decode_queries.shape[2]
    assert HEAD_DIM % width == 0
    factor = 1.0 / math.sqrt(HEAD_DIM)
    query_heads = decode_queries[0].reshape(requests, HEADS, HEAD_DIM)
    key_table = cache_keys[0].reshape(groups, reach, HEADS, HEAD_DIM)
    value_table = cache_values[0].reshape(groups, reach, HEADS, HEAD_DIM)
    scores = (
        jnp.einsum("rhd,gjhd->grhj", query_heads, key_table, preferred_element_type=jnp.float32)
        * factor
    )
    positions = tensor_rank * reach + jnp.arange(reach, dtype=jnp.int32)
    member = group_of[0][None, :] == jnp.arange(groups, dtype=jnp.int32)[:, None]
    within = positions[None, :] < cache_lengths[0][:, None]
    visible = (member[:, :, None] & within[:, None, :])[:, :, None, :]
    own_keys = new_keys[0].astype(jnp.float32).reshape(requests, HEADS, HEAD_DIM)
    own_score = jnp.sum(query_heads.astype(jnp.float32) * own_keys, axis=2) * factor
    local_peak = jnp.maximum(jnp.max(jnp.where(visible, scores, -jnp.inf), axis=(0, 3)), own_score)
    expon = jnp.where(visible, jnp.exp(scores - local_peak[None, :, :, None]), 0.0)
    probs = expon.astype(jnp.bfloat16)
    local_totals = jnp.sum(expon, axis=(0, 3))
    mixture = jnp.einsum(
        "grhj,gjhd->rhd", probs, value_table, preferred_element_type=jnp.float32
    ).reshape(requests, tensor_count, width)
    head_of = (jnp.arange(tensor_count, dtype=jnp.int32) * width) // HEAD_DIM
    peak_to = local_peak.T[head_of]
    totals_to = local_totals.T[head_of]
    flat_mix = jnp.transpose(mixture, (1, 0, 2)).reshape(tensor_count, requests * width)
    payload = jnp.concatenate([flat_mix, peak_to, totals_to], axis=1)
    return payload, own_score


def attention_finish(payload, own_score, new_values, decode_residual, out_weight):
    tensor_count = lax.axis_size("tensor")
    tensor_rank = lax.axis_index("tensor")
    requests, model_width = new_values.shape[1], new_values.shape[2]
    width = out_weight.shape[0]
    received = lax.all_to_all(payload, "tensor", 0, 0, tiled=True)
    mixed_width = requests * width
    part_mix = received[:, :mixed_width].reshape(tensor_count, requests, width)
    part_peak = received[:, mixed_width:mixed_width + requests]
    part_totals = received[:, mixed_width + requests:]
    peak = jnp.max(part_peak, axis=0)
    scale = jnp.exp(part_peak - peak[None, :])
    my_head = (tensor_rank * width) // HEAD_DIM
    first_column = tensor_rank * width
    own_here = lax.dynamic_index_in_dim(own_score, my_head, axis=1, keepdims=False)
    own_exp = jnp.exp(own_here - peak)
    own_prob = lax.optimization_barrier(own_exp.astype(jnp.bfloat16)).astype(jnp.float32)
    totals = jnp.sum(scale * part_totals, axis=0) + own_exp
    own_values = lax.dynamic_slice_in_dim(new_values[0], first_column, width, 1).astype(jnp.float32)
    summed_mix = jnp.sum(scale[:, :, None] * part_mix, axis=0) + own_prob[:, None] * own_values
    attended = (summed_mix / totals[:, None]).astype(jnp.bfloat16)
    partial = jnp.dot(attended, out_weight, preferred_element_type=jnp.float32)
    per_device = requests // tensor_count
    gathered = lax.all_to_all(
        partial.reshape(tensor_count, per_device, model_width), "tensor", 0, 0, tiled=True
    )
    projected = jnp.sum(gathered, axis=0)
    return (decode_residual[0].astype(jnp.float32) + projected).astype(jnp.bfloat16)


def rms_normed(residual_rows, norm_gain):
    row_float = residual_rows.astype(jnp.float32)
    inverse = lax.rsqrt(jnp.mean(row_float * row_float, axis=1, keepdims=True) + 1e-06)
    return row_float, (row_float * inverse * norm_gain).astype(jnp.bfloat16)


def dispatch(normed, slot_index, slot_count):
    row_count = normed.shape[0]
    slots = jnp.arange(slot_count, dtype=jnp.int32)
    select = jnp.any(
        slot_index.reshape(row_count, -1)[None, :, :] == slots[:, None, None], axis=2
    ).astype(jnp.bfloat16)
    outgoing = jnp.dot(select, normed, preferred_element_type=jnp.float32).astype(jnp.bfloat16)
    tensor_count = lax.axis_size("tensor")
    outgoing = outgoing.reshape(tensor_count, slot_count // tensor_count, normed.shape[1])
    return lax.all_to_all(outgoing, "tensor", split_axis=0, concat_axis=0, tiled=True)


def experts_on(received, experts, norm_gain):
    block = lax.all_gather(received, "dp", axis=0, tiled=True)
    _, normed = rms_normed(block.reshape(-1, block.shape[-1]), norm_gain)
    return expert_mlp(normed, *experts).reshape(block.shape).astype(jnp.bfloat16)


def rank_in_expert(flat_expert, tensor_count):
    one_hot = (flat_expert[:, None] == jnp.arange(tensor_count, dtype=jnp.int32)[None, :]).astype(
        jnp.int32
    )
    count = flat_expert.shape[0]
    lower = (
        jnp.arange(count, dtype=jnp.int32)[:, None] > jnp.arange(count, dtype=jnp.int32)[None, :]
    ).astype(jnp.bfloat16)
    earlier = jnp.dot(
        lower, one_hot.astype(jnp.bfloat16), preferred_element_type=jnp.float32
    ).astype(jnp.int32)
    return jnp.sum(earlier * one_hot, axis=1), jnp.sum(one_hot, axis=0)


def give_back(done):
    return lax.all_to_all(
        lax.psum_scatter(done, "dp", scatter_dimension=0, tiled=True),
        "tensor",
        split_axis=0,
        concat_axis=0,
        tiled=True,
    )


def per_device(
    decode_queries,
    new_keys,
    new_values,
    cache_keys,
    cache_values,
    group_of,
    cache_lengths,
    decode_residual,
    out_weight,
    prefill_states,
    norm_gain,
    routes,
    route_weights,
    w_gate,
    w_up,
    w_down,
):
    tensor_count = lax.axis_size("tensor")
    model_width = decode_queries.shape[2]
    prefill_count = prefill_states.shape[0]
    row_count, top_count = routes.shape
    decode_count = row_count - prefill_count
    capacity = max(8, (row_count * top_count * 3 // (2 * tensor_count) + 7) // 8 * 8)
    early = max(8, capacity * 2 // 3 // 8 * 8)
    late = max(capacity - early, decode_count)
    stride = early + late
    experts = (w_gate[0], w_up[0], w_down[0])
    prefill_routes = routes[:prefill_count].reshape(-1)
    decode_routes = routes[prefill_count:].reshape(-1)
    prefill_rank, prefill_counts = rank_in_expert(prefill_routes, tensor_count)
    decode_rank, _ = rank_in_expert(decode_routes, tensor_count)
    overflow = jnp.maximum(prefill_counts - early, 0)
    prefill_float = prefill_states.astype(jnp.float32)
    first_in = dispatch(
        prefill_states,
        jnp.where(prefill_rank < early, prefill_routes * early + prefill_rank, -1),
        tensor_count * early,
    )
    payload, own_score = attention_partials(
        decode_queries, new_keys, cache_keys, cache_values, group_of, cache_lengths,
        out_weight.shape[0],
    )
    payload, first_in = lax.optimization_barrier((payload, first_in))
    first_done = experts_on(first_in, experts, norm_gain)
    decode_hidden = attention_finish(payload, own_score, new_values, decode_residual, out_weight)
    decode_float = decode_hidden.astype(jnp.float32)
    late_slot = jnp.concatenate(
        [
            jnp.where(
                prefill_rank >= early, prefill_routes * late + prefill_rank - early, -1
            ),
            decode_routes * late + overflow[decode_routes] + decode_rank,
        ]
    )
    second_in = dispatch(
        jnp.concatenate([prefill_states, decode_hidden], axis=0), late_slot, tensor_count * late
    )
    first_done, second_in = lax.optimization_barrier((first_done, second_in))
    first_back = give_back(first_done)
    second_done = experts_on(second_in, experts, norm_gain)
    first_back, second_done = lax.optimization_barrier((first_back, second_done))
    second_back = give_back(second_done)
    returned = jnp.concatenate([first_back, second_back], axis=1).reshape(
        tensor_count * stride, model_width
    )
    place = jnp.concatenate(
        [
            prefill_routes * stride + prefill_rank,
            decode_routes * stride + early + overflow[decode_routes] + decode_rank,
        ]
    ).reshape(row_count, top_count)
    columns = jnp.arange(tensor_count * stride, dtype=jnp.int32)
    mixing = jnp.sum(
        jnp.where(place[:, :, None] == columns[None, None, :], route_weights[:, :, None], 0.0),
        axis=1,
    )
    high = mixing.astype(jnp.bfloat16)
    rest = mixing - high.astype(jnp.float32)
    middle = rest.astype(jnp.bfloat16)
    low = (rest - middle.astype(jnp.float32)).astype(jnp.bfloat16)

    def combined(lo, hi, row_float):
        parts = jnp.dot(
            jnp.concatenate([high[lo:hi], middle[lo:hi], low[lo:hi]], axis=0),
            returned,
            preferred_element_type=jnp.float32,
        ).reshape(3, hi - lo, model_width)
        weighted = (parts[0] + parts[1]) + parts[2]
        return (row_float + weighted).astype(jnp.bfloat16)

    return (
        combined(0, prefill_count, prefill_float),
        combined(prefill_count, row_count, decode_float)[None],
    )


def solution(mesh):
    in_specs = (
        P("dp", None, None),
        P("dp", None, None),
        P("dp", None, None),
        P("dp", None, "tensor", None),
        P("dp", None, "tensor", None),
        P("dp", None),
        P("dp", None),
        P("dp", "tensor", None),
        P("tensor", None),
        P(("dp", "tensor"), None),
        P(),
        P(("dp", "tensor"), None),
        P(("dp", "tensor"), None),
        P("tensor", None, "dp"),
        P("tensor", None, "dp"),
        P("tensor", "dp", None),
    )
    out_specs = (P(("dp", "tensor"), None), P("dp", "tensor", None))
    return jax.shard_map(
        per_device, mesh=mesh, in_specs=in_specs, out_specs=out_specs, check_vma=False
    )
```

```python
import math

import jax
import jax.numpy as jnp
from jax import lax
from jax.sharding import PartitionSpec as P

HEADS = 16
HEAD_DIM = 128


def expert_mlp(inputs, gate_w, up_w, down_w):
    flat_rows = inputs.reshape(-1, inputs.shape[-1])
    gate = jnp.dot(flat_rows, gate_w, preferred_element_type=jnp.float32)
    upper = jnp.dot(flat_rows, up_w, preferred_element_type=jnp.float32)
    active = (jax.nn.silu(gate) * upper).astype(jnp.bfloat16)
    return jnp.dot(active, down_w, preferred_element_type=jnp.float32)


def attention_partials(
    decode_queries, new_keys, cache_keys, cache_values, group_of, cache_lengths, width
):
    tensor_count = lax.axis_size("tensor")
    tensor_rank = lax.axis_index("tensor")
    requests = decode_queries.shape[1]
    groups = cache_keys.shape[1]
    reach = cache_keys.shape[2]
    model_width = decode_queries.shape[2]
    assert HEAD_DIM % width == 0
    factor = 1.0 / math.sqrt(HEAD_DIM)
    query_heads = decode_queries[0].reshape(requests, HEADS, HEAD_DIM)
    key_table = cache_keys[0].reshape(groups, reach, HEADS, HEAD_DIM)
    value_table = cache_values[0].reshape(groups, reach, HEADS, HEAD_DIM)
    scores = (
        jnp.einsum("rhd,gjhd->grhj", query_heads, key_table, preferred_element_type=jnp.float32)
        * factor
    )
    positions = tensor_rank * reach + jnp.arange(reach, dtype=jnp.int32)
    member = group_of[0][None, :] == jnp.arange(groups, dtype=jnp.int32)[:, None]
    within = positions[None, :] < cache_lengths[0][:, None]
    visible = (member[:, :, None] & within[:, None, :])[:, :, None, :]
    own_keys = new_keys[0].astype(jnp.float32).reshape(requests, HEADS, HEAD_DIM)
    own_score = jnp.sum(query_heads.astype(jnp.float32) * own_keys, axis=2) * factor
    local_peak = jnp.maximum(jnp.max(jnp.where(visible, scores, -jnp.inf), axis=(0, 3)), own_score)
    expon = jnp.where(visible, jnp.exp(scores - local_peak[None, :, :, None]), 0.0)
    probs = expon.astype(jnp.bfloat16)
    local_totals = jnp.sum(expon, axis=(0, 3))
    mixture = jnp.einsum(
        "grhj,gjhd->rhd", probs, value_table, preferred_element_type=jnp.float32
    ).reshape(requests, tensor_count, width)
    head_of = (jnp.arange(tensor_count, dtype=jnp.int32) * width) // HEAD_DIM
    peak_to = local_peak.T[head_of]
    totals_to = local_totals.T[head_of]
    flat_mix = jnp.transpose(mixture, (1, 0, 2)).reshape(tensor_count, requests * width)
    payload = jnp.concatenate([flat_mix, peak_to, totals_to], axis=1)
    return payload, own_score


def attention_finish(payload, own_score, new_values, decode_residual, out_weight):
    tensor_count = lax.axis_size("tensor")
    tensor_rank = lax.axis_index("tensor")
    requests, model_width = new_values.shape[1], new_values.shape[2]
    width = out_weight.shape[0]
    received = lax.all_to_all(payload, "tensor", 0, 0, tiled=True)
    mixed_width = requests * width
    part_mix = received[:, :mixed_width].reshape(tensor_count, requests, width)
    part_peak = received[:, mixed_width:mixed_width + requests]
    part_totals = received[:, mixed_width + requests:]
    peak = jnp.max(part_peak, axis=0)
    scale = jnp.exp(part_peak - peak[None, :])
    my_head = (tensor_rank * width) // HEAD_DIM
    first_column = tensor_rank * width
    own_here = lax.dynamic_index_in_dim(own_score, my_head, axis=1, keepdims=False)
    own_exp = jnp.exp(own_here - peak)
    own_prob = lax.optimization_barrier(own_exp.astype(jnp.bfloat16)).astype(jnp.float32)
    totals = jnp.sum(scale * part_totals, axis=0) + own_exp
    own_values = lax.dynamic_slice_in_dim(new_values[0], first_column, width, 1).astype(jnp.float32)
    summed_mix = jnp.sum(scale[:, :, None] * part_mix, axis=0) + own_prob[:, None] * own_values
    attended = (summed_mix / totals[:, None]).astype(jnp.bfloat16)
    lanes = 128
    partial = jnp.einsum(
        "rc,ctl->rtl", attended, out_weight.reshape(width, model_width // lanes, lanes),
        preferred_element_type=jnp.float32,
    )
    per_device = requests // tensor_count
    gathered = lax.all_to_all(
        partial.astype(jnp.bfloat16).reshape(
            tensor_count, per_device * (model_width // lanes), lanes
        ),
        "tensor", 0, 0, tiled=True,
    )
    projected = jnp.sum(
        gathered.astype(jnp.float32).reshape(tensor_count, per_device, model_width), axis=0
    )
    return (decode_residual[0].astype(jnp.float32) + projected).astype(jnp.bfloat16)


def rms_normed(residual_rows, norm_gain):
    row_float = residual_rows.astype(jnp.float32)
    inverse = lax.rsqrt(jnp.mean(row_float * row_float, axis=1, keepdims=True) + 1e-06)
    return row_float, (row_float * inverse * norm_gain).astype(jnp.bfloat16)


def dispatch(normed, slot_index, slot_count):
    row_count = normed.shape[0]
    slots = jnp.arange(slot_count, dtype=jnp.int32)
    select = jnp.any(
        slot_index.reshape(row_count, -1)[None, :, :] == slots[:, None, None], axis=2
    ).astype(jnp.bfloat16)
    outgoing = jnp.dot(select, normed, preferred_element_type=jnp.float32).astype(jnp.bfloat16)
    tensor_count = lax.axis_size("tensor")
    outgoing = outgoing.reshape(tensor_count, slot_count // tensor_count, normed.shape[1])
    return lax.all_to_all(outgoing, "tensor", split_axis=0, concat_axis=0, tiled=True)


def experts_on(received, experts, norm_gain):
    block = lax.all_gather(received, "dp", axis=0, tiled=True)
    _, normed = rms_normed(block.reshape(-1, block.shape[-1]), norm_gain)
    return expert_mlp(normed, *experts).reshape(block.shape).astype(jnp.bfloat16)


def rank_in_expert(flat_expert, tensor_count):
    one_hot = (flat_expert[:, None] == jnp.arange(tensor_count, dtype=jnp.int32)[None, :]).astype(
        jnp.int32
    )
    count = flat_expert.shape[0]
    lower = (
        jnp.arange(count, dtype=jnp.int32)[:, None] > jnp.arange(count, dtype=jnp.int32)[None, :]
    ).astype(jnp.bfloat16)
    earlier = jnp.dot(
        lower, one_hot.astype(jnp.bfloat16), preferred_element_type=jnp.float32
    ).astype(jnp.int32)
    return jnp.sum(earlier * one_hot, axis=1), jnp.sum(one_hot, axis=0)


def give_back(done):
    return lax.all_to_all(
        lax.psum_scatter(done, "dp", scatter_dimension=0, tiled=True),
        "tensor",
        split_axis=0,
        concat_axis=0,
        tiled=True,
    )


def per_device(
    decode_queries,
    new_keys,
    new_values,
    cache_keys,
    cache_values,
    group_of,
    cache_lengths,
    decode_residual,
    out_weight,
    prefill_states,
    norm_gain,
    routes,
    route_weights,
    w_gate,
    w_up,
    w_down,
):
    tensor_count = lax.axis_size("tensor")
    model_width = decode_queries.shape[2]
    prefill_count = prefill_states.shape[0]
    row_count, top_count = routes.shape
    decode_count = row_count - prefill_count
    capacity = max(8, (row_count * top_count * 3 // (2 * tensor_count) + 7) // 8 * 8)
    early = max(8, capacity * 2 // 3 // 8 * 8)
    late = max(capacity - early, decode_count)
    stride = early + late
    experts = (w_gate[0], w_up[0], w_down[0])
    prefill_routes = routes[:prefill_count].reshape(-1)
    decode_routes = routes[prefill_count:].reshape(-1)
    prefill_rank, prefill_counts = rank_in_expert(prefill_routes, tensor_count)
    decode_rank, _ = rank_in_expert(decode_routes, tensor_count)
    overflow = jnp.maximum(prefill_counts - early, 0)
    prefill_float = prefill_states.astype(jnp.float32)
    first_in = dispatch(
        prefill_states,
        jnp.where(prefill_rank < early, prefill_routes * early + prefill_rank, -1),
        tensor_count * early,
    )
    payload, own_score = attention_partials(
        decode_queries, new_keys, cache_keys, cache_values, group_of, cache_lengths,
        out_weight.shape[0],
    )
    payload, first_in = lax.optimization_barrier((payload, first_in))
    first_done = experts_on(first_in, experts, norm_gain)
    decode_hidden = attention_finish(payload, own_score, new_values, decode_residual, out_weight)
    decode_float = decode_hidden.astype(jnp.float32)
    late_slot = jnp.concatenate(
        [
            jnp.where(
                prefill_rank >= early, prefill_routes * late + prefill_rank - early, -1
            ),
            decode_routes * late + overflow[decode_routes] + decode_rank,
        ]
    )
    second_in = dispatch(
        jnp.concatenate([prefill_states, decode_hidden], axis=0), late_slot, tensor_count * late
    )
    first_done, second_in = lax.optimization_barrier((first_done, second_in))
    first_back = give_back(first_done)
    second_done = experts_on(second_in, experts, norm_gain)
    first_back, second_done = lax.optimization_barrier((first_back, second_done))
    second_back = give_back(second_done)
    returned = jnp.concatenate([first_back, second_back], axis=1).reshape(
        tensor_count * stride, model_width
    )
    place = jnp.concatenate(
        [
            prefill_routes * stride + prefill_rank,
            decode_routes * stride + early + overflow[decode_routes] + decode_rank,
        ]
    ).reshape(row_count, top_count)
    columns = jnp.arange(tensor_count * stride, dtype=jnp.int32)
    mixing = jnp.sum(
        jnp.where(place[:, :, None] == columns[None, None, :], route_weights[:, :, None], 0.0),
        axis=1,
    )
    high = mixing.astype(jnp.bfloat16)
    rest = mixing - high.astype(jnp.float32)
    middle = rest.astype(jnp.bfloat16)
    low = (rest - middle.astype(jnp.float32)).astype(jnp.bfloat16)

    def combined(lo, hi, row_float):
        parts = jnp.dot(
            jnp.concatenate([high[lo:hi], middle[lo:hi], low[lo:hi]], axis=0),
            returned,
            preferred_element_type=jnp.float32,
        ).reshape(3, hi - lo, model_width)
        weighted = (parts[0] + parts[1]) + parts[2]
        return (row_float + weighted).astype(jnp.bfloat16)

    return (
        combined(0, prefill_count, prefill_float),
        combined(prefill_count, row_count, decode_float)[None],
    )


def solution(mesh):
    in_specs = (
        P("dp", None, None),
        P("dp", None, None),
        P("dp", None, None),
        P("dp", None, "tensor", None),
        P("dp", None, "tensor", None),
        P("dp", None),
        P("dp", None),
        P("dp", "tensor", None),
        P("tensor", None),
        P(("dp", "tensor"), None),
        P(),
        P(("dp", "tensor"), None),
        P(("dp", "tensor"), None),
        P("tensor", None, "dp"),
        P("tensor", None, "dp"),
        P("tensor", "dp", None),
    )
    out_specs = (P(("dp", "tensor"), None), P("dp", "tensor", None))
    return jax.shard_map(
        per_device, mesh=mesh, in_specs=in_specs, out_specs=out_specs, check_vma=False
    )
```

```python
import math

import jax
import jax.numpy as jnp
from jax import lax
from jax.sharding import PartitionSpec as P

HEADS = 16
HEAD_DIM = 128


def expert_mlp(inputs, gate_w, up_w, down_w):
    flat_rows = inputs.reshape(-1, inputs.shape[-1])
    gate = jnp.dot(flat_rows, gate_w, preferred_element_type=jnp.float32)
    upper = jnp.dot(flat_rows, up_w, preferred_element_type=jnp.float32)
    active = (jax.nn.silu(gate) * upper).astype(jnp.bfloat16)
    return jnp.dot(active, down_w, preferred_element_type=jnp.float32)


def attention_partials(
    decode_queries, new_keys, cache_keys, cache_values, group_of, cache_lengths, width
):
    tensor_count = lax.axis_size("tensor")
    tensor_rank = lax.axis_index("tensor")
    requests = decode_queries.shape[1]
    groups = cache_keys.shape[1]
    reach = cache_keys.shape[2]
    model_width = decode_queries.shape[2]
    assert HEAD_DIM % width == 0
    factor = 1.0 / math.sqrt(HEAD_DIM)
    query_heads = decode_queries[0].reshape(requests, HEADS, HEAD_DIM)
    key_table = cache_keys[0].reshape(groups, reach, HEADS, HEAD_DIM)
    value_table = cache_values[0].reshape(groups, reach, HEADS, HEAD_DIM)
    scores = (
        jnp.einsum("rhd,gjhd->grhj", query_heads, key_table, preferred_element_type=jnp.float32)
        * factor
    )
    positions = tensor_rank * reach + jnp.arange(reach, dtype=jnp.int32)
    member = group_of[0][None, :] == jnp.arange(groups, dtype=jnp.int32)[:, None]
    within = positions[None, :] < cache_lengths[0][:, None]
    visible = (member[:, :, None] & within[:, None, :])[:, :, None, :]
    own_keys = new_keys[0].astype(jnp.float32).reshape(requests, HEADS, HEAD_DIM)
    own_score = jnp.sum(query_heads.astype(jnp.float32) * own_keys, axis=2) * factor
    local_peak = jnp.maximum(jnp.max(jnp.where(visible, scores, -jnp.inf), axis=(0, 3)), own_score)
    expon = jnp.where(visible, jnp.exp(scores - local_peak[None, :, :, None]), 0.0)
    probs = expon.astype(jnp.bfloat16)
    local_totals = jnp.sum(expon, axis=(0, 3))
    mixture = jnp.einsum(
        "grhj,gjhd->rhd", probs, value_table, preferred_element_type=jnp.float32
    ).reshape(requests, tensor_count, width)
    head_of = (jnp.arange(tensor_count, dtype=jnp.int32) * width) // HEAD_DIM
    peak_to = local_peak.T[head_of]
    totals_to = local_totals.T[head_of]
    flat_mix = jnp.transpose(mixture, (1, 0, 2)).reshape(tensor_count, requests * width)
    payload = jnp.concatenate([flat_mix, peak_to, totals_to], axis=1)
    return payload, own_score


def attention_finish(payload, own_score, new_values, decode_residual, out_weight):
    tensor_count = lax.axis_size("tensor")
    tensor_rank = lax.axis_index("tensor")
    requests, model_width = new_values.shape[1], new_values.shape[2]
    width = out_weight.shape[0]
    received = lax.all_to_all(payload, "tensor", 0, 0, tiled=True)
    mixed_width = requests * width
    part_mix = received[:, :mixed_width].reshape(tensor_count, requests, width)
    part_peak = received[:, mixed_width:mixed_width + requests]
    part_totals = received[:, mixed_width + requests:]
    peak = jnp.max(part_peak, axis=0)
    scale = jnp.exp(part_peak - peak[None, :])
    my_head = (tensor_rank * width) // HEAD_DIM
    first_column = tensor_rank * width
    own_here = lax.dynamic_index_in_dim(own_score, my_head, axis=1, keepdims=False)
    own_exp = jnp.exp(own_here - peak)
    own_prob = lax.optimization_barrier(own_exp.astype(jnp.bfloat16)).astype(jnp.float32)
    totals = jnp.sum(scale * part_totals, axis=0) + own_exp
    own_values = lax.dynamic_slice_in_dim(new_values[0], first_column, width, 1).astype(jnp.float32)
    summed_mix = jnp.sum(scale[:, :, None] * part_mix, axis=0) + own_prob[:, None] * own_values
    attended = (summed_mix / totals[:, None]).astype(jnp.bfloat16)
    lanes = 128
    partial = jnp.einsum(
        "rc,ctl->rtl", attended, out_weight.reshape(width, model_width // lanes, lanes),
        preferred_element_type=jnp.float32,
    )
    per_device = requests // tensor_count
    gathered = lax.all_to_all(
        partial.astype(jnp.bfloat16).reshape(
            tensor_count, per_device * (model_width // lanes), lanes
        ),
        "tensor", 0, 0, tiled=True,
    )
    projected = jnp.sum(
        gathered.astype(jnp.float32).reshape(tensor_count, per_device, model_width), axis=0
    )
    return (decode_residual[0].astype(jnp.float32) + projected).astype(jnp.bfloat16)


def rms_normed(residual_rows, norm_gain):
    row_float = residual_rows.astype(jnp.float32)
    inverse = lax.rsqrt(jnp.mean(row_float * row_float, axis=1, keepdims=True) + 1e-06)
    return row_float, (row_float * inverse * norm_gain).astype(jnp.bfloat16)


def dispatch(normed, slot_index, slot_count):
    row_count = normed.shape[0]
    slots = jnp.arange(slot_count, dtype=jnp.int32)
    select = jnp.any(
        slot_index.reshape(row_count, -1)[None, :, :] == slots[:, None, None], axis=2
    ).astype(jnp.bfloat16)
    select = lax.optimization_barrier(select)
    outgoing = jnp.dot(select, normed, preferred_element_type=jnp.float32).astype(jnp.bfloat16)
    tensor_count = lax.axis_size("tensor")
    outgoing = outgoing.reshape(tensor_count, slot_count // tensor_count, normed.shape[1])
    return lax.all_to_all(outgoing, "tensor", split_axis=0, concat_axis=0, tiled=True)


def experts_on(received, experts, norm_gain):
    block = lax.all_gather(received, "dp", axis=0, tiled=True)
    _, normed = rms_normed(block.reshape(-1, block.shape[-1]), norm_gain)
    return expert_mlp(normed, *experts).reshape(block.shape).astype(jnp.bfloat16)


def rank_in_expert(flat_expert, tensor_count):
    one_hot = (flat_expert[:, None] == jnp.arange(tensor_count, dtype=jnp.int32)[None, :]).astype(
        jnp.int32
    )
    count = flat_expert.shape[0]
    lower = (
        jnp.arange(count, dtype=jnp.int32)[:, None] > jnp.arange(count, dtype=jnp.int32)[None, :]
    ).astype(jnp.bfloat16)
    earlier = jnp.dot(
        lower, one_hot.astype(jnp.bfloat16), preferred_element_type=jnp.float32
    ).astype(jnp.int32)
    return jnp.sum(earlier * one_hot, axis=1), jnp.sum(one_hot, axis=0)


def give_back(done):
    return lax.all_to_all(
        lax.psum_scatter(done, "dp", scatter_dimension=0, tiled=True),
        "tensor",
        split_axis=0,
        concat_axis=0,
        tiled=True,
    )


def per_device(
    decode_queries,
    new_keys,
    new_values,
    cache_keys,
    cache_values,
    group_of,
    cache_lengths,
    decode_residual,
    out_weight,
    prefill_states,
    norm_gain,
    routes,
    route_weights,
    w_gate,
    w_up,
    w_down,
):
    tensor_count = lax.axis_size("tensor")
    model_width = decode_queries.shape[2]
    prefill_count = prefill_states.shape[0]
    row_count, top_count = routes.shape
    decode_count = row_count - prefill_count
    capacity = max(8, (row_count * top_count * 3 // (2 * tensor_count) + 7) // 8 * 8)
    early = max(8, capacity * 2 // 3 // 8 * 8)
    late = max(capacity - early, decode_count)
    stride = early + late
    experts = (w_gate[0], w_up[0], w_down[0])
    prefill_routes = routes[:prefill_count].reshape(-1)
    decode_routes = routes[prefill_count:].reshape(-1)
    prefill_rank, prefill_counts = rank_in_expert(prefill_routes, tensor_count)
    decode_rank, _ = rank_in_expert(decode_routes, tensor_count)
    overflow = jnp.maximum(prefill_counts - early, 0)
    prefill_float = prefill_states.astype(jnp.float32)
    first_in = dispatch(
        prefill_states,
        jnp.where(prefill_rank < early, prefill_routes * early + prefill_rank, -1),
        tensor_count * early,
    )
    payload, own_score = attention_partials(
        decode_queries, new_keys, cache_keys, cache_values, group_of, cache_lengths,
        out_weight.shape[0],
    )
    payload, first_in = lax.optimization_barrier((payload, first_in))
    first_done = experts_on(first_in, experts, norm_gain)
    decode_hidden = attention_finish(payload, own_score, new_values, decode_residual, out_weight)
    decode_float = decode_hidden.astype(jnp.float32)
    late_slot = jnp.concatenate(
        [
            jnp.where(
                prefill_rank >= early, prefill_routes * late + prefill_rank - early, -1
            ),
            decode_routes * late + overflow[decode_routes] + decode_rank,
        ]
    )
    second_in = dispatch(
        jnp.concatenate([prefill_states, decode_hidden], axis=0), late_slot, tensor_count * late
    )
    first_done, second_in = lax.optimization_barrier((first_done, second_in))
    first_back = give_back(first_done)
    second_done = experts_on(second_in, experts, norm_gain)
    first_back, second_done = lax.optimization_barrier((first_back, second_done))
    second_back = give_back(second_done)
    returned = jnp.concatenate([first_back, second_back], axis=1).reshape(
        tensor_count * stride, model_width
    )
    place = jnp.concatenate(
        [
            prefill_routes * stride + prefill_rank,
            decode_routes * stride + early + overflow[decode_routes] + decode_rank,
        ]
    ).reshape(row_count, top_count)
    columns = jnp.arange(tensor_count * stride, dtype=jnp.int32)
    mixing = jnp.sum(
        jnp.where(place[:, :, None] == columns[None, None, :], route_weights[:, :, None], 0.0),
        axis=1,
    )
    high = mixing.astype(jnp.bfloat16)
    rest = mixing - high.astype(jnp.float32)
    middle = rest.astype(jnp.bfloat16)
    low = (rest - middle.astype(jnp.float32)).astype(jnp.bfloat16)

    def combined(lo, hi, row_float):
        parts = jnp.dot(
            jnp.concatenate([high[lo:hi], middle[lo:hi], low[lo:hi]], axis=0),
            returned,
            preferred_element_type=jnp.float32,
        ).reshape(3, hi - lo, model_width)
        weighted = (parts[0] + parts[1]) + parts[2]
        return (row_float + weighted).astype(jnp.bfloat16)

    return (
        combined(0, prefill_count, prefill_float),
        combined(prefill_count, row_count, decode_float)[None],
    )


def solution(mesh):
    in_specs = (
        P("dp", None, None),
        P("dp", None, None),
        P("dp", None, None),
        P("dp", None, "tensor", None),
        P("dp", None, "tensor", None),
        P("dp", None),
        P("dp", None),
        P("dp", "tensor", None),
        P("tensor", None),
        P(("dp", "tensor"), None),
        P(),
        P(("dp", "tensor"), None),
        P(("dp", "tensor"), None),
        P("tensor", None, "dp"),
        P("tensor", None, "dp"),
        P("tensor", "dp", None),
    )
    out_specs = (P(("dp", "tensor"), None), P("dp", "tensor", None))
    return jax.shard_map(
        per_device, mesh=mesh, in_specs=in_specs, out_specs=out_specs, check_vma=False
    )
```

```python
import math

import jax
import jax.numpy as jnp
from jax import lax
from jax.sharding import PartitionSpec as P

HEADS = 16
HEAD_DIM = 128


def expert_mlp(inputs, gate_w, up_w, down_w):
    flat_rows = inputs.reshape(-1, inputs.shape[-1])
    gate = jnp.dot(flat_rows, gate_w, preferred_element_type=jnp.float32)
    upper = jnp.dot(flat_rows, up_w, preferred_element_type=jnp.float32)
    active = (jax.nn.silu(gate) * upper).astype(jnp.bfloat16)
    return jnp.dot(active, down_w, preferred_element_type=jnp.float32)


def attention_partials(
    decode_queries, new_keys, cache_keys, cache_values, group_of, cache_lengths, width
):
    tensor_count = lax.axis_size("tensor")
    tensor_rank = lax.axis_index("tensor")
    requests = decode_queries.shape[1]
    groups = cache_keys.shape[1]
    reach = cache_keys.shape[2]
    model_width = decode_queries.shape[2]
    assert HEAD_DIM % width == 0
    factor = 1.0 / math.sqrt(HEAD_DIM)
    query_heads = decode_queries[0].reshape(requests, HEADS, HEAD_DIM)
    key_table = cache_keys[0].reshape(groups, reach, HEADS, HEAD_DIM)
    value_table = cache_values[0].reshape(groups, reach, HEADS, HEAD_DIM)
    scores = (
        jnp.einsum("rhd,gjhd->grhj", query_heads, key_table, preferred_element_type=jnp.float32)
        * factor
    )
    positions = tensor_rank * reach + jnp.arange(reach, dtype=jnp.int32)
    member = group_of[0][None, :] == jnp.arange(groups, dtype=jnp.int32)[:, None]
    within = positions[None, :] < cache_lengths[0][:, None]
    visible = (member[:, :, None] & within[:, None, :])[:, :, None, :]
    own_keys = new_keys[0].astype(jnp.float32).reshape(requests, HEADS, HEAD_DIM)
    own_score = jnp.sum(query_heads.astype(jnp.float32) * own_keys, axis=2) * factor
    local_peak = jnp.maximum(jnp.max(jnp.where(visible, scores, -jnp.inf), axis=(0, 3)), own_score)
    expon = jnp.where(visible, jnp.exp(scores - local_peak[None, :, :, None]), 0.0)
    probs = expon.astype(jnp.bfloat16)
    local_totals = jnp.sum(expon, axis=(0, 3))
    mixture = jnp.einsum(
        "grhj,gjhd->rhd", probs, value_table, preferred_element_type=jnp.float32
    ).reshape(requests, tensor_count, width)
    head_of = (jnp.arange(tensor_count, dtype=jnp.int32) * width) // HEAD_DIM
    peak_to = local_peak.T[head_of]
    totals_to = local_totals.T[head_of]
    flat_mix = jnp.transpose(mixture, (1, 0, 2)).reshape(tensor_count, requests * width)
    payload = jnp.concatenate([flat_mix, peak_to, totals_to], axis=1)
    return payload, own_score


def attention_finish(payload, own_score, new_values, decode_residual, out_weight):
    tensor_count = lax.axis_size("tensor")
    tensor_rank = lax.axis_index("tensor")
    requests, model_width = new_values.shape[1], new_values.shape[2]
    width = out_weight.shape[0]
    received = lax.all_to_all(payload, "tensor", 0, 0, tiled=True)
    mixed_width = requests * width
    part_mix = received[:, :mixed_width].reshape(tensor_count, requests, width)
    part_peak = received[:, mixed_width:mixed_width + requests]
    part_totals = received[:, mixed_width + requests:]
    peak = jnp.max(part_peak, axis=0)
    scale = jnp.exp(part_peak - peak[None, :])
    my_head = (tensor_rank * width) // HEAD_DIM
    first_column = tensor_rank * width
    own_here = lax.dynamic_index_in_dim(own_score, my_head, axis=1, keepdims=False)
    own_exp = jnp.exp(own_here - peak)
    own_prob = lax.optimization_barrier(own_exp.astype(jnp.bfloat16)).astype(jnp.float32)
    totals = jnp.sum(scale * part_totals, axis=0) + own_exp
    own_values = lax.dynamic_slice_in_dim(new_values[0], first_column, width, 1).astype(jnp.float32)
    summed_mix = jnp.sum(scale[:, :, None] * part_mix, axis=0) + own_prob[:, None] * own_values
    attended = (summed_mix / totals[:, None]).astype(jnp.bfloat16)
    lanes = 128
    partial = jnp.einsum(
        "rc,ctl->rtl", attended, out_weight.reshape(width, model_width // lanes, lanes),
        preferred_element_type=jnp.float32,
    )
    per_device = requests // tensor_count
    gathered = lax.all_to_all(
        partial.astype(jnp.bfloat16).reshape(
            tensor_count, per_device * (model_width // lanes), lanes
        ),
        "tensor", 0, 0, tiled=True,
    )
    projected = jnp.sum(
        gathered.astype(jnp.float32).reshape(tensor_count, per_device, model_width), axis=0
    )
    return (decode_residual[0].astype(jnp.float32) + projected).astype(jnp.bfloat16)


def rms_normed(residual_rows, norm_gain):
    row_float = residual_rows.astype(jnp.float32)
    inverse = lax.rsqrt(jnp.mean(row_float * row_float, axis=1, keepdims=True) + 1e-06)
    return row_float, (row_float * inverse * norm_gain).astype(jnp.bfloat16)


def dispatch(normed, slot_index, slot_count):
    row_count = normed.shape[0]
    slots = jnp.arange(slot_count, dtype=jnp.int32)
    select = jnp.any(
        slot_index.reshape(row_count, -1)[None, :, :] == slots[:, None, None], axis=2
    ).astype(jnp.bfloat16)
    numbers = jnp.arange(1, row_count + 1, dtype=jnp.float32).astype(jnp.bfloat16)
    which = jnp.dot(select, numbers, preferred_element_type=jnp.float32).astype(jnp.int32) - 1
    which = jnp.where(which < 0, row_count, which)
    outgoing = jnp.take(normed, which, axis=0, mode="fill", fill_value=0).astype(jnp.bfloat16)
    tensor_count = lax.axis_size("tensor")
    outgoing = outgoing.reshape(tensor_count, slot_count // tensor_count, normed.shape[1])
    return lax.all_to_all(outgoing, "tensor", split_axis=0, concat_axis=0, tiled=True)


def experts_on(received, experts, norm_gain):
    block = lax.all_gather(received, "dp", axis=0, tiled=True)
    _, normed = rms_normed(block.reshape(-1, block.shape[-1]), norm_gain)
    return expert_mlp(normed, *experts).reshape(block.shape).astype(jnp.bfloat16)


def rank_in_expert(flat_expert, tensor_count):
    one_hot = (flat_expert[:, None] == jnp.arange(tensor_count, dtype=jnp.int32)[None, :]).astype(
        jnp.int32
    )
    count = flat_expert.shape[0]
    lower = (
        jnp.arange(count, dtype=jnp.int32)[:, None] > jnp.arange(count, dtype=jnp.int32)[None, :]
    ).astype(jnp.bfloat16)
    earlier = jnp.dot(
        lower, one_hot.astype(jnp.bfloat16), preferred_element_type=jnp.float32
    ).astype(jnp.int32)
    return jnp.sum(earlier * one_hot, axis=1), jnp.sum(one_hot, axis=0)


def give_back(done):
    return lax.all_to_all(
        lax.psum_scatter(done, "dp", scatter_dimension=0, tiled=True),
        "tensor",
        split_axis=0,
        concat_axis=0,
        tiled=True,
    )


def per_device(
    decode_queries,
    new_keys,
    new_values,
    cache_keys,
    cache_values,
    group_of,
    cache_lengths,
    decode_residual,
    out_weight,
    prefill_states,
    norm_gain,
    routes,
    route_weights,
    w_gate,
    w_up,
    w_down,
):
    tensor_count = lax.axis_size("tensor")
    model_width = decode_queries.shape[2]
    prefill_count = prefill_states.shape[0]
    row_count, top_count = routes.shape
    decode_count = row_count - prefill_count
    capacity = max(8, (row_count * top_count * 3 // (2 * tensor_count) + 7) // 8 * 8)
    early = max(8, capacity * 2 // 3 // 8 * 8)
    late = max(capacity - early, decode_count)
    stride = early + late
    experts = (w_gate[0], w_up[0], w_down[0])
    prefill_routes = routes[:prefill_count].reshape(-1)
    decode_routes = routes[prefill_count:].reshape(-1)
    prefill_rank, prefill_counts = rank_in_expert(prefill_routes, tensor_count)
    decode_rank, _ = rank_in_expert(decode_routes, tensor_count)
    overflow = jnp.maximum(prefill_counts - early, 0)
    prefill_float = prefill_states.astype(jnp.float32)
    first_in = dispatch(
        prefill_states,
        jnp.where(prefill_rank < early, prefill_routes * early + prefill_rank, -1),
        tensor_count * early,
    )
    payload, own_score = attention_partials(
        decode_queries, new_keys, cache_keys, cache_values, group_of, cache_lengths,
        out_weight.shape[0],
    )
    payload, first_in = lax.optimization_barrier((payload, first_in))
    first_done = experts_on(first_in, experts, norm_gain)
    decode_hidden = attention_finish(payload, own_score, new_values, decode_residual, out_weight)
    decode_float = decode_hidden.astype(jnp.float32)
    late_slot = jnp.concatenate(
        [
            jnp.where(
                prefill_rank >= early, prefill_routes * late + prefill_rank - early, -1
            ),
            decode_routes * late + overflow[decode_routes] + decode_rank,
        ]
    )
    second_in = dispatch(
        jnp.concatenate([prefill_states, decode_hidden], axis=0), late_slot, tensor_count * late
    )
    first_done, second_in = lax.optimization_barrier((first_done, second_in))
    first_back = give_back(first_done)
    second_done = experts_on(second_in, experts, norm_gain)
    first_back, second_done = lax.optimization_barrier((first_back, second_done))
    second_back = give_back(second_done)
    returned = jnp.concatenate([first_back, second_back], axis=1).reshape(
        tensor_count * stride, model_width
    )
    place = jnp.concatenate(
        [
            prefill_routes * stride + prefill_rank,
            decode_routes * stride + early + overflow[decode_routes] + decode_rank,
        ]
    ).reshape(row_count, top_count)
    columns = jnp.arange(tensor_count * stride, dtype=jnp.int32)
    mixing = jnp.sum(
        jnp.where(place[:, :, None] == columns[None, None, :], route_weights[:, :, None], 0.0),
        axis=1,
    )
    high = mixing.astype(jnp.bfloat16)
    rest = mixing - high.astype(jnp.float32)
    middle = rest.astype(jnp.bfloat16)
    low = (rest - middle.astype(jnp.float32)).astype(jnp.bfloat16)

    def combined(lo, hi, row_float):
        parts = jnp.dot(
            jnp.concatenate([high[lo:hi], middle[lo:hi], low[lo:hi]], axis=0),
            returned,
            preferred_element_type=jnp.float32,
        ).reshape(3, hi - lo, model_width)
        weighted = (parts[0] + parts[1]) + parts[2]
        return (row_float + weighted).astype(jnp.bfloat16)

    return (
        combined(0, prefill_count, prefill_float),
        combined(prefill_count, row_count, decode_float)[None],
    )


def solution(mesh):
    in_specs = (
        P("dp", None, None),
        P("dp", None, None),
        P("dp", None, None),
        P("dp", None, "tensor", None),
        P("dp", None, "tensor", None),
        P("dp", None),
        P("dp", None),
        P("dp", "tensor", None),
        P("tensor", None),
        P(("dp", "tensor"), None),
        P(),
        P(("dp", "tensor"), None),
        P(("dp", "tensor"), None),
        P("tensor", None, "dp"),
        P("tensor", None, "dp"),
        P("tensor", "dp", None),
    )
    out_specs = (P(("dp", "tensor"), None), P("dp", "tensor", None))
    return jax.shard_map(
        per_device, mesh=mesh, in_specs=in_specs, out_specs=out_specs, check_vma=False
    )
```

```python
import math

import jax
import jax.numpy as jnp
from jax import lax
from jax.sharding import PartitionSpec as P

HEADS = 16
HEAD_DIM = 128


def expert_mlp(inputs, gate_w, up_w, down_w):
    flat_rows = inputs.reshape(-1, inputs.shape[-1])
    gate = jnp.dot(flat_rows, gate_w, preferred_element_type=jnp.float32)
    upper = jnp.dot(flat_rows, up_w, preferred_element_type=jnp.float32)
    active = (jax.nn.silu(gate) * upper).astype(jnp.bfloat16)
    return jnp.dot(active, down_w, preferred_element_type=jnp.float32)


def attention_partials(
    decode_queries, new_keys, cache_keys, cache_values, group_of, cache_lengths, width
):
    tensor_count = lax.axis_size("tensor")
    tensor_rank = lax.axis_index("tensor")
    requests = decode_queries.shape[1]
    groups = cache_keys.shape[1]
    reach = cache_keys.shape[2]
    model_width = decode_queries.shape[2]
    assert HEAD_DIM % width == 0
    factor = 1.0 / math.sqrt(HEAD_DIM)
    query_heads = decode_queries[0].reshape(requests, HEADS, HEAD_DIM)
    key_table = cache_keys[0].reshape(groups, reach, HEADS, HEAD_DIM)
    value_table = cache_values[0].reshape(groups, reach, HEADS, HEAD_DIM)
    scores = (
        jnp.einsum("rhd,gjhd->grhj", query_heads, key_table, preferred_element_type=jnp.float32)
        * factor
    )
    positions = tensor_rank * reach + jnp.arange(reach, dtype=jnp.int32)
    member = group_of[0][None, :] == jnp.arange(groups, dtype=jnp.int32)[:, None]
    within = positions[None, :] < cache_lengths[0][:, None]
    visible = (member[:, :, None] & within[:, None, :])[:, :, None, :]
    own_keys = new_keys[0].astype(jnp.float32).reshape(requests, HEADS, HEAD_DIM)
    own_score = jnp.sum(query_heads.astype(jnp.float32) * own_keys, axis=2) * factor
    local_peak = jnp.maximum(jnp.max(jnp.where(visible, scores, -jnp.inf), axis=(0, 3)), own_score)
    expon = jnp.where(visible, jnp.exp(scores - local_peak[None, :, :, None]), 0.0)
    probs = expon.astype(jnp.bfloat16)
    local_totals = jnp.sum(expon, axis=(0, 3))
    mixture = jnp.einsum(
        "grhj,gjhd->rhd", probs, value_table, preferred_element_type=jnp.float32
    ).reshape(requests, tensor_count, width)
    head_of = (jnp.arange(tensor_count, dtype=jnp.int32) * width) // HEAD_DIM
    peak_to = local_peak.T[head_of]
    totals_to = local_totals.T[head_of]
    flat_mix = jnp.transpose(mixture, (1, 0, 2)).reshape(tensor_count, requests * width)
    payload = jnp.concatenate([flat_mix, peak_to, totals_to], axis=1)
    return payload, own_score


def attention_finish(payload, own_score, new_values, decode_residual, out_weight):
    tensor_count = lax.axis_size("tensor")
    tensor_rank = lax.axis_index("tensor")
    requests, model_width = new_values.shape[1], new_values.shape[2]
    width = out_weight.shape[0]
    received = lax.all_to_all(payload, "tensor", 0, 0, tiled=True)
    mixed_width = requests * width
    part_mix = received[:, :mixed_width].reshape(tensor_count, requests, width)
    part_peak = received[:, mixed_width:mixed_width + requests]
    part_totals = received[:, mixed_width + requests:]
    peak = jnp.max(part_peak, axis=0)
    scale = jnp.exp(part_peak - peak[None, :])
    my_head = (tensor_rank * width) // HEAD_DIM
    first_column = tensor_rank * width
    own_here = lax.dynamic_index_in_dim(own_score, my_head, axis=1, keepdims=False)
    own_exp = jnp.exp(own_here - peak)
    own_prob = lax.optimization_barrier(own_exp.astype(jnp.bfloat16)).astype(jnp.float32)
    totals = jnp.sum(scale * part_totals, axis=0) + own_exp
    own_values = lax.dynamic_slice_in_dim(new_values[0], first_column, width, 1).astype(jnp.float32)
    summed_mix = jnp.sum(scale[:, :, None] * part_mix, axis=0) + own_prob[:, None] * own_values
    attended = (summed_mix / totals[:, None]).astype(jnp.bfloat16)
    lanes = 128
    partial = jnp.einsum(
        "rc,ctl->rtl", attended, out_weight.reshape(width, model_width // lanes, lanes),
        preferred_element_type=jnp.float32,
    )
    per_device = requests // tensor_count
    gathered = lax.all_to_all(
        partial.astype(jnp.bfloat16).reshape(
            tensor_count, per_device * (model_width // lanes), lanes
        ),
        "tensor", 0, 0, tiled=True,
    )
    projected = jnp.sum(
        gathered.astype(jnp.float32).reshape(tensor_count, per_device, model_width), axis=0
    )
    return (decode_residual[0].astype(jnp.float32) + projected).astype(jnp.bfloat16)


def rms_normed(residual_rows, norm_gain):
    row_float = residual_rows.astype(jnp.float32)
    inverse = lax.rsqrt(jnp.mean(row_float * row_float, axis=1, keepdims=True) + 1e-06)
    return row_float, (row_float * inverse * norm_gain).astype(jnp.bfloat16)


def dispatch(normed, slot_index, slot_count):
    row_count = normed.shape[0]
    slots = jnp.arange(slot_count, dtype=jnp.int32)
    select = jnp.any(
        slot_index.reshape(row_count, -1)[None, :, :] == slots[:, None, None], axis=2
    ).astype(jnp.bfloat16)
    select = lax.optimization_barrier(select)
    outgoing = jnp.dot(select, normed, preferred_element_type=jnp.float32).astype(jnp.bfloat16)
    tensor_count = lax.axis_size("tensor")
    outgoing = outgoing.reshape(tensor_count, slot_count // tensor_count, normed.shape[1])
    return lax.all_to_all(outgoing, "tensor", split_axis=0, concat_axis=0, tiled=True)


def experts_on(received, experts, norm_gain):
    block = lax.all_gather(received, "dp", axis=0, tiled=True)
    _, normed = rms_normed(block.reshape(-1, block.shape[-1]), norm_gain)
    return expert_mlp(normed, *experts).reshape(block.shape).astype(jnp.bfloat16)


def rank_in_expert(flat_expert, tensor_count):
    one_hot = (flat_expert[:, None] == jnp.arange(tensor_count, dtype=jnp.int32)[None, :]).astype(
        jnp.int32
    )
    count = flat_expert.shape[0]
    lower = (
        jnp.arange(count, dtype=jnp.int32)[:, None] > jnp.arange(count, dtype=jnp.int32)[None, :]
    ).astype(jnp.bfloat16)
    earlier = jnp.dot(
        lower, one_hot.astype(jnp.bfloat16), preferred_element_type=jnp.float32
    ).astype(jnp.int32)
    return jnp.sum(earlier * one_hot, axis=1), jnp.sum(one_hot, axis=0)


def give_back(done):
    return lax.all_to_all(
        lax.psum_scatter(done, "dp", scatter_dimension=0, tiled=True),
        "tensor",
        split_axis=0,
        concat_axis=0,
        tiled=True,
    )


def per_device(
    decode_queries,
    new_keys,
    new_values,
    cache_keys,
    cache_values,
    group_of,
    cache_lengths,
    decode_residual,
    out_weight,
    prefill_states,
    norm_gain,
    routes,
    route_weights,
    w_gate,
    w_up,
    w_down,
):
    tensor_count = lax.axis_size("tensor")
    model_width = decode_queries.shape[2]
    prefill_count = prefill_states.shape[0]
    row_count, top_count = routes.shape
    decode_count = row_count - prefill_count
    capacity = max(8, (row_count * top_count * 3 // (2 * tensor_count) + 7) // 8 * 8)
    early = max(8, capacity * 2 // 3 // 8 * 8)
    late = max(capacity - early, decode_count)
    stride = early + late
    experts = (w_gate[0], w_up[0], w_down[0])
    prefill_routes = routes[:prefill_count].reshape(-1)
    decode_routes = routes[prefill_count:].reshape(-1)
    prefill_rank, prefill_counts = rank_in_expert(prefill_routes, tensor_count)
    decode_rank, _ = rank_in_expert(decode_routes, tensor_count)
    overflow = jnp.maximum(prefill_counts - early, 0)
    prefill_float = prefill_states.astype(jnp.float32)
    first_in = dispatch(
        prefill_states,
        jnp.where(prefill_rank < early, prefill_routes * early + prefill_rank, -1),
        tensor_count * early,
    )
    payload, own_score = attention_partials(
        decode_queries, new_keys, cache_keys, cache_values, group_of, cache_lengths,
        out_weight.shape[0],
    )
    payload, first_in = lax.optimization_barrier((payload, first_in))
    first_done = experts_on(first_in, experts, norm_gain)
    decode_hidden = attention_finish(payload, own_score, new_values, decode_residual, out_weight)
    decode_float = decode_hidden.astype(jnp.float32)
    late_slot = jnp.concatenate(
        [
            jnp.where(
                prefill_rank >= early, prefill_routes * late + prefill_rank - early, -1
            ),
            decode_routes * late + overflow[decode_routes] + decode_rank,
        ]
    )
    second_in = dispatch(
        jnp.concatenate([prefill_states, decode_hidden], axis=0), late_slot, tensor_count * late
    )
    first_done, second_in = lax.optimization_barrier((first_done, second_in))
    first_back = give_back(first_done)
    second_done = experts_on(second_in, experts, norm_gain)
    first_back, second_done = lax.optimization_barrier((first_back, second_done))
    second_back = give_back(second_done)
    first_back = first_back.reshape(tensor_count * early, model_width)
    second_back = second_back.reshape(tensor_count * late, model_width)
    place = jnp.concatenate(
        [
            prefill_routes * stride + prefill_rank,
            decode_routes * stride + early + overflow[decode_routes] + decode_rank,
        ]
    ).reshape(row_count, top_count)
    columns = jnp.arange(tensor_count * stride, dtype=jnp.int32)
    mixing = jnp.sum(
        jnp.where(place[:, :, None] == columns[None, None, :], route_weights[:, :, None], 0.0),
        axis=1,
    )
    high = mixing.astype(jnp.bfloat16)
    rest = mixing - high.astype(jnp.float32)
    middle = rest.astype(jnp.bfloat16)
    low = (rest - middle.astype(jnp.float32)).astype(jnp.bfloat16)

    def combined(lo, hi, row_float):
        weights = jnp.concatenate([high[lo:hi], middle[lo:hi], low[lo:hi]], axis=0).reshape(
            3 * (hi - lo), tensor_count, stride
        )
        parts = (
            jnp.dot(
                weights[:, :, :early].reshape(3 * (hi - lo), tensor_count * early),
                first_back,
                preferred_element_type=jnp.float32,
            )
            + jnp.dot(
                weights[:, :, early:].reshape(3 * (hi - lo), tensor_count * late),
                second_back,
                preferred_element_type=jnp.float32,
            )
        ).reshape(3, hi - lo, model_width)
        weighted = (parts[0] + parts[1]) + parts[2]
        return (row_float + weighted).astype(jnp.bfloat16)

    return (
        combined(0, prefill_count, prefill_float),
        combined(prefill_count, row_count, decode_float)[None],
    )


def solution(mesh):
    in_specs = (
        P("dp", None, None),
        P("dp", None, None),
        P("dp", None, None),
        P("dp", None, "tensor", None),
        P("dp", None, "tensor", None),
        P("dp", None),
        P("dp", None),
        P("dp", "tensor", None),
        P("tensor", None),
        P(("dp", "tensor"), None),
        P(),
        P(("dp", "tensor"), None),
        P(("dp", "tensor"), None),
        P("tensor", None, "dp"),
        P("tensor", None, "dp"),
        P("tensor", "dp", None),
    )
    out_specs = (P(("dp", "tensor"), None), P("dp", "tensor", None))
    return jax.shard_map(
        per_device, mesh=mesh, in_specs=in_specs, out_specs=out_specs, check_vma=False
    )
```
